512 devices in a mesh: space: 32 (over z_lo, x), scal: 16 (over y, z_hi, core).
Axes of the slice: x: 4, y: 4, z: 16 (z_hi: 2, z_lo: 8; z = z_hi * 8 + z_lo), core: 2. Of those that a mesh axis runs over, the one named last changes fastest.
Arguments:
- scalars: float32 [512, 2048, 256], P('scal', 'space'), may hold values from -6 to 6
- schmidt: float32 [512], P('scal'), may hold values from 1 to 1000
- velocity_history: bfloat16 [32, 2, 256, 256], P('scal', None, 'space'), may hold values from -0.796875 to 0.796875
- fine_src: int32 [2048], replicated, may hold values from 0 to 254, as said below
- remap_weight: float32 [2048], replicated, may hold values from 0 to 1
- snap_step: int32 [2], replicated, may hold values from 0 to 31
Outputs:
- transported: float32 [512, 2048, 256], P('scal', 'space')
The draws below stay inside these ranges and needn't reach their ends.
Inputs may be any that keep to these rules, and one draw needn't show every extreme that they name: fine_src may name any coarse row of any tile, in no particular order.
All inputs are finite; a program needn't handle non-finite values.
Results may differ from the reference program's by a relative error of at most 0.0003.
Values may be sent and summed in bfloat16 or wider, within the bound.
No kernel may reach another device: no remote copies, remote signals or barrier semaphores. Data moves between devices by JAX's collectives and lax.ppermute only.
A program may use at most 64 MiB of HBM per device.

```python
import math
import jax
import jax.numpy as jnp
from jax import lax

SC_DEV = 32
TX = 64
NZ = 256
CR_DEV = 8
STEPS = 2
NSCAL = 512
NX = 2048
NCX = 256
NSNAP = 32
N_SCAL = 16


def draw_fine_src(key, part):
    tile_count = NX // TX
    tile_id = jnp.arange(tile_count, dtype=jnp.int32)
    column = jnp.arange(TX, dtype=jnp.int32)
    rows = jax.random.randint(jax.random.fold_in(key, 17), (tile_count, TX), 0, NCX - 1).astype(jnp.int32)
    within = jax.random.randint(jax.random.fold_in(key, 29), (tile_count, 3), 0, CR_DEV).astype(jnp.int32)
    far_tile = (tile_id + tile_count // 2) % tile_count
    before_tile = (tile_id + tile_count - 1) % tile_count
    after_tile = (tile_id + 1) % tile_count
    far_row = jnp.minimum(far_tile * CR_DEV + within[:, 0], NCX - 2)
    before_row = jnp.minimum(before_tile * CR_DEV + within[:, 1], NCX - 2)
    after_row = jnp.minimum(after_tile * CR_DEV + within[:, 2], NCX - 2)
    rows = jnp.where(column[None, :] == 0, far_row[:, None], rows)
    rows = jnp.where(column[None, :] == 1, before_row[:, None], rows)
    rows = jnp.where(column[None, :] == 2, after_row[:, None], rows)
    edge_first = (column[None, :] == 3) & (tile_id[:, None] == 0)
    edge_last = (column[None, :] == 3) & (tile_id[:, None] == tile_count - 1)
    rows = jnp.where(edge_first, NCX - 2, rows)
    rows = jnp.where(edge_last, 0, rows)
    return rows.reshape(NX).astype(jnp.int32)


def shard_levels(key, extent, pieces, least, largest):
    def one(dim, parts):
        heights = jax.random.uniform(jax.random.fold_in(jax.random.fold_in(key, 6), dim), (parts,), jnp.float32, least / len(pieces), largest / len(pieces))
        return jnp.repeat(jnp.exp(heights), extent[dim] // parts).reshape((-1,) + (1,) * (len(extent) - dim - 1))

    loudness = one(*pieces[0])
    for cut in pieces[1:]:
        loudness = loudness * one(*cut)
    return loudness


def gaussian(key, dims, spread, reach, cuts=(), held_as=jnp.bfloat16):
    level = shard_levels(key, dims, cuts, -0.22, 0.18) if cuts else 1.0
    drawn = jax.random.normal(key, dims, jnp.float32) * spread * level
    return jnp.minimum(jnp.maximum(drawn, -reach), reach).astype(held_as)


def setup_inputs(seed: int = 0) -> dict:
    streams_of = jax.random.split(jax.random.key(seed), 7)
    scalars = gaussian(streams_of[0], (NSCAL, NX, NZ), 1.0, 6.0, ((0, 16), (1, 32)), jnp.float32)
    schmidt = jnp.clip(jnp.exp(math.log(1000.0) - 6.9077553 * jax.random.uniform(streams_of[1], (NSCAL,), jnp.float32) ** shard_levels(streams_of[1], (NSCAL,), ((0, 16),), -0.2, 0.2)), 1.0, 1000.0)
    velocity_history = gaussian(streams_of[2], (NSNAP, 2, NCX, NZ), 0.2, 0.796875, ((0, 16), (2, 32)))
    fine_src = draw_fine_src(jax.random.fold_in(streams_of[6], 71), 0)
    remap_weight = jnp.clip(jax.random.uniform(streams_of[4], (NX,), jnp.float32, 0.0, 1.0), 0.0, 1.0)
    snap_step = jax.random.randint(streams_of[5], (STEPS,), 0, NSNAP).astype(jnp.int32)
    return dict(scalars=scalars, schmidt=schmidt, velocity_history=velocity_history, fine_src=fine_src, remap_weight=remap_weight, snap_step=snap_step)


diffusion_scale = 0.24


def advance(padded, velocity, diffusivity):
    center = padded[:, 1:-1]
    upper_row = padded[:, 2:]
    lower_row = padded[:, :-2]
    east_cell = jnp.roll(center, -1, axis=2)
    west_cell = jnp.roll(center, 1, axis=2)
    laplacian = upper_row + lower_row + east_cell + west_cell - 4.0 * center
    return (center - velocity[0] * (0.5 * (upper_row - lower_row))
            - velocity[1] * (0.5 * (east_cell - west_cell))
            + diffusivity[:, None, None] * laplacian)


def remap_snapshot(coarse, fine_src, remap_weight):
    coarse = coarse.astype(jnp.float32)
    lower_pick = coarse[:, fine_src]
    upper_pick = coarse[:, fine_src + 1]
    return lower_pick * (1.0 - remap_weight)[None, :, None] + upper_pick * remap_weight[None, :, None]


def reference(scalars, schmidt, velocity_history, fine_src, remap_weight, snap_step):
    diffusivity = diffusion_scale / schmidt
    velocities = [remap_snapshot(lax.dynamic_index_in_dim(velocity_history, snap_step[step_index], 0, keepdims=False), fine_src, remap_weight) for step_index in range(STEPS)]

    def one_group(operands):
        field, group_diff = operands
        for step_index in range(STEPS):
            padded = jnp.pad(field, ((0, 0), (1, 1), (0, 0)))
            field = advance(padded, velocities[step_index], group_diff)
        return field

    shaped = scalars.reshape(N_SCAL, SC_DEV, NX, NZ)
    result = lax.map(one_group, (shaped, diffusivity.reshape(N_SCAL, SC_DEV)))
    return result.reshape(NSCAL, NX, NZ)
```

```python
import jax
import jax.numpy as jnp
from jax import lax
from jax.sharding import PartitionSpec as P

STEPS = 2


diffusion_scale = 0.24


def radices(count):
    out = []
    while count > 4 and count % 4 == 0 and count // 4 >= 4:
        out.append(4)
        count //= 4
    if count > 1:
        out.append(count)
    return out


def shift_pairs(count, stride, radix, k):
    pairs = []
    for i in range(count):
        d = (i // stride) % radix
        pairs.append((i, i + (((d + k) % radix) - d) * stride))
    return pairs


def candidates(value, axis, stride, radix):
    count = lax.axis_size(axis)
    out = [value]
    for k in range(1, radix):
        out.append(lax.ppermute(value, axis, shift_pairs(count, stride, radix, k)))
    return jnp.stack(out)


def from_owners(block, owners, slots, axis):
    me = lax.axis_index(axis)
    stride = 1
    for round_index, radix in enumerate(radices(lax.axis_size(axis))):
        digit = (me // stride) % radix
        cands = candidates(block, axis, stride, radix)
        picked = []
        for step_index in range(owners.shape[0]):
            want = (owners[step_index] // stride) % radix
            one = lax.dynamic_index_in_dim(cands, (digit - want) % radix, 0, keepdims=False)
            if round_index == 0:
                one = lax.dynamic_index_in_dim(one, slots[step_index], 0, keepdims=False)
            else:
                one = one[step_index]
            picked.append(one)
        block = jnp.stack(picked)
        stride *= radix
    return block


def gather_blocks(block, axis):
    me = lax.axis_index(axis)
    count = lax.axis_size(axis)
    stride = 1
    for radix in radices(count):
        digit = (me // stride) % radix
        cands = candidates(block, axis, stride, radix)
        order = (digit - jnp.arange(radix, dtype=jnp.int32)) % radix
        block = jnp.take(cands, order, axis=0)
        if stride > 1:
            block = block.reshape((radix * block.shape[1],) + block.shape[2:])
        stride *= radix
    return block


def advance(padded, velocity, diffusivity):
    center = padded[:, 1:-1]
    upper_row = padded[:, 2:]
    lower_row = padded[:, :-2]
    east_cell = jnp.roll(center, -1, axis=2)
    west_cell = jnp.roll(center, 1, axis=2)
    laplacian = upper_row + lower_row + east_cell + west_cell - 4.0 * center
    return (
        center
        - velocity[0] * (0.5 * (upper_row - lower_row))
        - velocity[1] * (0.5 * (east_cell - west_cell))
        + diffusivity[:, None, None] * laplacian
    )


def remap(coarse, rows, weights):
    lower_pick = jnp.take(coarse, rows, axis=1)
    upper_pick = jnp.take(coarse, rows + 1, axis=1)
    return lower_pick * (1.0 - weights)[None, :, None] + upper_pick * weights[None, :, None]


def body(scalars, schmidt, velocity_history, fine_src, remap_weight, snap_step):
    tile_rows = scalars.shape[1]
    snap_dev = velocity_history.shape[0]
    tile_count = lax.axis_size("space")
    me = lax.axis_index("space")
    anchor = me * tile_rows
    diffusivity = diffusion_scale / schmidt

    width = STEPS
    head = scalars[:, :width]
    tail = scalars[:, tile_rows - width:]
    below = lax.ppermute(tail, "space", [(i, i + 1) for i in range(tile_count - 1)])
    above = lax.ppermute(head, "space", [(i + 1, i) for i in range(tile_count - 1)])
    field = jnp.concatenate([below, scalars, above], axis=1)

    owners = snap_step // snap_dev
    slots = snap_step % snap_dev
    local = from_owners(velocity_history, owners, slots, "scal")
    gathered = gather_blocks(local, "space")
    gathered = gathered.reshape((tile_count,) + local.shape)
    coarse = jnp.moveaxis(gathered, 0, 2)
    coarse = coarse.reshape(
        coarse.shape[:2] + (coarse.shape[2] * coarse.shape[3],) + coarse.shape[4:]
    ).astype(jnp.float32)

    padded_src = jnp.pad(fine_src, (width, width))
    padded_weight = jnp.pad(remap_weight, (width, width))
    row_index = jnp.arange(tile_rows + 2 * width, dtype=jnp.int32) + anchor - width
    for step_index in range(STEPS):
        extra = width - step_index - 1
        count = tile_rows + 2 * extra
        rows = lax.dynamic_slice_in_dim(padded_src, anchor + width - extra, count)
        weights = lax.dynamic_slice_in_dim(padded_weight, anchor + width - extra, count)
        velocity = remap(coarse[step_index], rows, weights)
        field = advance(field, velocity, diffusivity)
        if extra > 0:
            inside = lax.dynamic_slice_in_dim(row_index, width - extra, count)
            inside = (inside >= 0) & (inside < tile_rows * tile_count)
            field = jnp.where(inside[None, :, None], field, 0.0)
    return field


def solution(mesh):
    return jax.shard_map(
        body,
        mesh=mesh,
        in_specs=(
            P("scal", "space", None),
            P("scal"),
            P("scal", None, "space", None),
            P(),
            P(),
            P(),
        ),
        out_specs=P("scal", "space", None),
        check_vma=False,
    )
```

```python
import jax
import jax.numpy as jnp
from jax import lax
from jax.sharding import PartitionSpec as P

STEPS = 2


diffusion_scale = 0.24


def exchange(value, axis):
    count = lax.axis_size(axis)
    spread = jnp.broadcast_to(value[None], (count,) + value.shape)
    return lax.all_to_all(spread, axis, 0, 0, tiled=False)


def advance(padded, velocity, diffusivity):
    center = padded[:, 1:-1]
    upper_row = padded[:, 2:]
    lower_row = padded[:, :-2]
    east_cell = jnp.roll(center, -1, axis=2)
    west_cell = jnp.roll(center, 1, axis=2)
    laplacian = upper_row + lower_row + east_cell + west_cell - 4.0 * center
    return (
        center
        - velocity[0] * (0.5 * (upper_row - lower_row))
        - velocity[1] * (0.5 * (east_cell - west_cell))
        + diffusivity[:, None, None] * laplacian
    )


def remap(coarse, rows, weights):
    lower_pick = jnp.take(coarse, rows, axis=1)
    upper_pick = jnp.take(coarse, rows + 1, axis=1)
    return lower_pick * (1.0 - weights)[None, :, None] + upper_pick * weights[None, :, None]


def body(scalars, schmidt, velocity_history, fine_src, remap_weight, snap_step):
    tile_rows = scalars.shape[1]
    snap_dev = velocity_history.shape[0]
    tile_count = lax.axis_size("space")
    me = lax.axis_index("space")
    anchor = me * tile_rows
    diffusivity = diffusion_scale / schmidt

    width = STEPS
    head = scalars[:, :width]
    tail = scalars[:, tile_rows - width:]
    below = lax.ppermute(tail, "space", [(i, i + 1) for i in range(tile_count - 1)])
    above = lax.ppermute(head, "space", [(i + 1, i) for i in range(tile_count - 1)])
    field = jnp.concatenate([below, scalars, above], axis=1)

    owners = snap_step // snap_dev
    slots = snap_step % snap_dev
    blocks = exchange(velocity_history, "scal")
    local = jnp.stack(
        [blocks[owners[step_index], slots[step_index]] for step_index in range(STEPS)]
    )
    gathered = exchange(local, "space")
    coarse = jnp.moveaxis(gathered, 0, 2)
    coarse = coarse.reshape(
        coarse.shape[:2] + (coarse.shape[2] * coarse.shape[3],) + coarse.shape[4:]
    ).astype(jnp.float32)

    padded_src = jnp.pad(fine_src, (width, width))
    padded_weight = jnp.pad(remap_weight, (width, width))
    row_index = jnp.arange(tile_rows + 2 * width, dtype=jnp.int32) + anchor - width
    for step_index in range(STEPS):
        extra = width - step_index - 1
        count = tile_rows + 2 * extra
        rows = lax.dynamic_slice_in_dim(padded_src, anchor + width - extra, count)
        weights = lax.dynamic_slice_in_dim(padded_weight, anchor + width - extra, count)
        velocity = remap(coarse[step_index], rows, weights)
        field = advance(field, velocity, diffusivity)
        if extra > 0:
            inside = lax.dynamic_slice_in_dim(row_index, width - extra, count)
            inside = (inside >= 0) & (inside < tile_rows * tile_count)
            field = jnp.where(inside[None, :, None], field, 0.0)
    return field


def solution(mesh):
    return jax.shard_map(
        body,
        mesh=mesh,
        in_specs=(
            P("scal", "space", None),
            P("scal"),
            P("scal", None, "space", None),
            P(),
            P(),
            P(),
        ),
        out_specs=P("scal", "space", None),
        check_vma=False,
    )
```

```python
import jax
import jax.numpy as jnp
from jax import lax
from jax.experimental import pallas as pl
from jax.experimental.pallas import tpu as pltpu
from jax.sharding import PartitionSpec as P

STEPS = 2


diffusion_scale = 0.24


def exchange(value, axis):
    count = lax.axis_size(axis)
    spread = jnp.broadcast_to(value[None], (count,) + value.shape)
    return lax.all_to_all(spread, axis, 0, 0, tiled=False)


def advance(center, upper_row, lower_row, velocity_0, velocity_1, diffusivity):
    east_cell = pltpu.roll(center, center.shape[1] - 1, 1)
    west_cell = pltpu.roll(center, 1, 1)
    laplacian = upper_row + lower_row + east_cell + west_cell - 4.0 * center
    return (
        center
        - velocity_0 * (0.5 * (upper_row - lower_row))
        - velocity_1 * (0.5 * (east_cell - west_cell))
        + diffusivity * laplacian
    )


def transport_kernel(
    diff_ref, src_ref, weight_ref, keep_ref,
    coarse_ref, below_ref, tile_ref, above_ref,
    out_ref,
    vel0_ref, vel1_ref, wide_ref, mid_ref,
):
    block = tile_ref.shape[0]
    rows = tile_ref.shape[1]
    halo = below_ref.shape[1]
    ext = rows + 2 * halo - 2

    @pl.when(pl.program_id(0) == 0)
    def _():
        def one_row(r, carry):
            src = src_ref[r]
            w = weight_ref[r]
            for comp in range(2):
                for step_index, vel_ref, shift in ((0, vel0_ref, 0), (1, vel1_ref, 1)):
                    lower = coarse_ref[step_index, comp, pl.ds(src, 1), :]
                    upper = coarse_ref[step_index, comp, pl.ds(src + 1, 1), :]
                    value = lower * (1.0 - w) + upper * w
                    if shift == 0:
                        vel_ref[comp, pl.ds(r, 1), :] = value
                    else:
                        @pl.when((r >= 1) & (r <= rows))
                        def _():
                            vel_ref[comp, pl.ds(r - 1, 1), :] = value
            return carry

        lax.fori_loop(0, ext, one_row, 0)

    row = lax.broadcasted_iota(jnp.int32, (ext, tile_ref.shape[2]), 0)
    keep = ((row != 0) | (keep_ref[0] != 0)) & ((row != ext - 1) | (keep_ref[1] != 0))
    for k in range(block):
        d = diff_ref[pl.program_id(0) * block + k]
        wide_ref[pl.ds(0, halo), :] = below_ref[k]
        wide_ref[pl.ds(halo, rows), :] = tile_ref[k]
        wide_ref[pl.ds(halo + rows, halo), :] = above_ref[k]
        first = advance(
            wide_ref[pl.ds(1, ext), :],
            wide_ref[pl.ds(2, ext), :],
            wide_ref[pl.ds(0, ext), :],
            vel0_ref[0], vel0_ref[1], d,
        )
        mid_ref[...] = jnp.where(keep, first, 0.0)
        out_ref[k] = advance(
            mid_ref[pl.ds(1, rows), :],
            mid_ref[pl.ds(2, rows), :],
            mid_ref[pl.ds(0, rows), :],
            vel1_ref[0], vel1_ref[1], d,
        )


def body(scalars, schmidt, velocity_history, fine_src, remap_weight, snap_step):
    scal_dev, tile_rows, cells = scalars.shape
    snap_dev = velocity_history.shape[0]
    tile_count = lax.axis_size("space")
    me = lax.axis_index("space")
    anchor = me * tile_rows
    diffusivity = diffusion_scale / schmidt

    width = STEPS
    head = scalars[:, :width]
    tail = scalars[:, tile_rows - width:]
    below = lax.ppermute(tail, "space", [(i, i + 1) for i in range(tile_count - 1)])
    above = lax.ppermute(head, "space", [(i + 1, i) for i in range(tile_count - 1)])

    owners = snap_step // snap_dev
    slots = snap_step % snap_dev
    blocks = exchange(velocity_history, "scal")
    local = jnp.stack(
        [blocks[owners[step_index], slots[step_index]] for step_index in range(STEPS)]
    )
    gathered = exchange(local, "space")
    coarse = jnp.moveaxis(gathered, 0, 2)
    coarse = coarse.reshape(
        coarse.shape[:2] + (coarse.shape[2] * coarse.shape[3],) + coarse.shape[4:]
    ).astype(jnp.float32)

    ext = tile_rows + 2 * (width - 1)
    padded_src = jnp.pad(fine_src, (1, 1))
    padded_weight = jnp.pad(remap_weight, (1, 1))
    src = lax.dynamic_slice_in_dim(padded_src, anchor, ext)
    weights = lax.dynamic_slice_in_dim(padded_weight, anchor, ext)
    keep = jnp.stack([me > 0, me < tile_count - 1]).astype(jnp.int32)

    block = 8 if scal_dev % 8 == 0 else 1
    smem = pl.BlockSpec(memory_space=pltpu.SMEM)
    halo_spec = pl.BlockSpec((block, width, cells), lambda i: (i, 0, 0))
    tile_spec = pl.BlockSpec((block, tile_rows, cells), lambda i: (i, 0, 0))
    return pl.pallas_call(
        transport_kernel,
        grid=(scal_dev // block,),
        in_specs=[
            smem, smem, smem, smem,
            pl.BlockSpec(coarse.shape, lambda i: (0, 0, 0, 0)),
            halo_spec, tile_spec, halo_spec,
        ],
        out_specs=tile_spec,
        out_shape=jax.ShapeDtypeStruct(scalars.shape, scalars.dtype),
        scratch_shapes=[
            pltpu.VMEM((2, ext, cells), jnp.float32),
            pltpu.VMEM((2, tile_rows, cells), jnp.float32),
            pltpu.VMEM((tile_rows + 2 * width, cells), jnp.float32),
            pltpu.VMEM((ext, cells), jnp.float32),
        ],
        compiler_params=pltpu.CompilerParams(dimension_semantics=("arbitrary",)),
    )(diffusivity, src, weights, keep, coarse, below, scalars, above)


def solution(mesh):
    return jax.shard_map(
        body,
        mesh=mesh,
        in_specs=(
            P("scal", "space", None),
            P("scal"),
            P("scal", None, "space", None),
            P(),
            P(),
            P(),
        ),
        out_specs=P("scal", "space", None),
        check_vma=False,
    )
```

```python
import jax
import jax.numpy as jnp
from jax import lax
from jax.experimental import pallas as pl
from jax.experimental.pallas import tpu as pltpu
from jax.sharding import PartitionSpec as P

STEPS = 2


diffusion_scale = 0.24


def exchange(value, axis):
    count = lax.axis_size(axis)
    spread = jnp.broadcast_to(value[None], (count,) + value.shape)
    return lax.all_to_all(spread, axis, 0, 0, tiled=False)


def advance(center, upper_row, lower_row, velocity_0, velocity_1, diffusivity):
    east_cell = pltpu.roll(center, center.shape[1] - 1, 1)
    west_cell = pltpu.roll(center, 1, 1)
    laplacian = upper_row + lower_row + east_cell + west_cell - 4.0 * center
    return (
        center
        - velocity_0 * (0.5 * (upper_row - lower_row))
        - velocity_1 * (0.5 * (east_cell - west_cell))
        + diffusivity * laplacian
    )


def transport_kernel(
    diff_ref, src_ref, weight_ref, keep_ref,
    coarse_ref, below_ref, tile_ref, above_ref,
    out_ref,
    vel0_ref, vel1_ref, wide_ref, mid_ref,
):
    block = tile_ref.shape[0]
    rows = tile_ref.shape[1]
    halo = below_ref.shape[1]
    ext = rows + 2 * halo - 2

    @pl.when(pl.program_id(0) == 0)
    def _():
        part = coarse_ref.shape[3]
        for r in range(ext):
            src = src_ref[r]
            w = weight_ref[r]
            low_tile, low_row = src // part, src % part
            high_tile, high_row = (src + 1) // part, (src + 1) % part
            for step_index, vel_ref, shift in ((0, vel0_ref, 0), (1, vel1_ref, 1)):
                at = r - shift
                if at < 0 or at >= vel_ref.shape[1]:
                    continue
                for comp in range(2):
                    lower = coarse_ref[low_tile, step_index, comp, pl.ds(low_row, 1), :]
                    upper = coarse_ref[high_tile, step_index, comp, pl.ds(high_row, 1), :]
                    vel_ref[comp, pl.ds(at, 1), :] = lower * (1.0 - w) + upper * w

    row = lax.broadcasted_iota(jnp.int32, (ext, tile_ref.shape[2]), 0)
    keep = ((row != 0) | (keep_ref[0] != 0)) & ((row != ext - 1) | (keep_ref[1] != 0))
    for k in range(block):
        d = diff_ref[pl.program_id(0) * block + k]
        wide_ref[pl.ds(0, halo), :] = below_ref[k]
        wide_ref[pl.ds(halo, rows), :] = tile_ref[k]
        wide_ref[pl.ds(halo + rows, halo), :] = above_ref[k]
        first = advance(
            wide_ref[pl.ds(1, ext), :],
            wide_ref[pl.ds(2, ext), :],
            wide_ref[pl.ds(0, ext), :],
            vel0_ref[0], vel0_ref[1], d,
        )
        mid_ref[...] = jnp.where(keep, first, 0.0)
        out_ref[k] = advance(
            mid_ref[pl.ds(1, rows), :],
            mid_ref[pl.ds(2, rows), :],
            mid_ref[pl.ds(0, rows), :],
            vel1_ref[0], vel1_ref[1], d,
        )


def body(scalars, schmidt, velocity_history, fine_src, remap_weight, snap_step):
    scal_dev, tile_rows, cells = scalars.shape
    snap_dev = velocity_history.shape[0]
    tile_count = lax.axis_size("space")
    me = lax.axis_index("space")
    anchor = me * tile_rows
    diffusivity = diffusion_scale / schmidt

    width = STEPS
    head = scalars[:, :width]
    tail = scalars[:, tile_rows - width:]
    below = lax.ppermute(tail, "space", [(i, i + 1) for i in range(tile_count - 1)])
    above = lax.ppermute(head, "space", [(i + 1, i) for i in range(tile_count - 1)])

    owners = snap_step // snap_dev
    slots = snap_step % snap_dev
    blocks = exchange(velocity_history, "scal")
    local = jnp.stack(
        [blocks[owners[step_index], slots[step_index]] for step_index in range(STEPS)]
    )
    gathered = exchange(local, "space")
    coarse = gathered.astype(jnp.float32)

    ext = tile_rows + 2 * (width - 1)
    padded_src = jnp.pad(fine_src, (1, 1))
    padded_weight = jnp.pad(remap_weight, (1, 1))
    src = lax.dynamic_slice_in_dim(padded_src, anchor, ext)
    weights = lax.dynamic_slice_in_dim(padded_weight, anchor, ext)
    keep = jnp.stack([me > 0, me < tile_count - 1]).astype(jnp.int32)

    block = 8 if scal_dev % 8 == 0 else 1
    smem = pl.BlockSpec(memory_space=pltpu.SMEM)
    halo_spec = pl.BlockSpec((block, width, cells), lambda i: (i, 0, 0))
    tile_spec = pl.BlockSpec((block, tile_rows, cells), lambda i: (i, 0, 0))
    return pl.pallas_call(
        transport_kernel,
        grid=(scal_dev // block,),
        in_specs=[
            smem, smem, smem, smem,
            pl.BlockSpec(coarse.shape, lambda i: (0,) * coarse.ndim),
            halo_spec, tile_spec, halo_spec,
        ],
        out_specs=tile_spec,
        out_shape=jax.ShapeDtypeStruct(scalars.shape, scalars.dtype),
        scratch_shapes=[
            pltpu.VMEM((2, ext, cells), jnp.float32),
            pltpu.VMEM((2, tile_rows, cells), jnp.float32),
            pltpu.VMEM((tile_rows + 2 * width, cells), jnp.float32),
            pltpu.VMEM((ext, cells), jnp.float32),
        ],
        compiler_params=pltpu.CompilerParams(dimension_semantics=("arbitrary",)),
    )(diffusivity, src, weights, keep, coarse, below, scalars, above)


def solution(mesh):
    return jax.shard_map(
        body,
        mesh=mesh,
        in_specs=(
            P("scal", "space", None),
            P("scal"),
            P("scal", None, "space", None),
            P(),
            P(),
            P(),
        ),
        out_specs=P("scal", "space", None),
        check_vma=False,
    )
```

```python
import jax
import jax.numpy as jnp
from jax import lax
from jax.experimental import pallas as pl
from jax.experimental.pallas import tpu as pltpu
from jax.sharding import PartitionSpec as P

STEPS = 2


diffusion_scale = 0.24


def exchange(value, axis):
    count = lax.axis_size(axis)
    spread = jnp.broadcast_to(value[None], (count,) + value.shape)
    return lax.all_to_all(spread, axis, 0, 0, tiled=False)


def advance(center, half_0, half_1, diffusivity):
    rows, cells = center.shape
    upper_row = pltpu.roll(center, rows - 1, 0)
    lower_row = pltpu.roll(center, 1, 0)
    east_cell = pltpu.roll(center, cells - 1, 1)
    west_cell = pltpu.roll(center, 1, 1)
    laplacian = upper_row + lower_row + east_cell + west_cell - 4.0 * center
    return (
        center
        - half_0 * (upper_row - lower_row)
        - half_1 * (east_cell - west_cell)
        + diffusivity * laplacian
    )


def transport_kernel(
    diff_ref, src_ref, weight_ref, keep_ref,
    coarse_ref, below_ref, tile_ref, above_ref,
    out_ref,
    half0_ref, half1_ref, wide_ref,
):
    block = tile_ref.shape[0]
    rows = tile_ref.shape[1]
    halo = below_ref.shape[1]
    frame = wide_ref.shape[0]
    pad = (frame - rows) // 2
    ext = src_ref.shape[0]

    @pl.when(pl.program_id(0) == 0)
    def _():
        wide_ref[...] = jnp.zeros_like(wide_ref)
        half0_ref[...] = jnp.zeros_like(half0_ref)
        half1_ref[...] = jnp.zeros_like(half1_ref)
        part = coarse_ref.shape[3]
        for r in range(ext):
            src = src_ref[r]
            w = weight_ref[r]
            low_tile, low_row = src // part, src % part
            high_tile, high_row = (src + 1) // part, (src + 1) % part
            for step_index, half_ref, first in ((0, half0_ref, 0), (1, half1_ref, 1)):
                if r < first or r >= ext - first:
                    continue
                at = pad - 1 + r
                for comp in range(2):
                    lower = coarse_ref[low_tile, step_index, comp, pl.ds(low_row, 1), :]
                    upper = coarse_ref[high_tile, step_index, comp, pl.ds(high_row, 1), :]
                    value = lower * (1.0 - w) + upper * w
                    half_ref[comp, pl.ds(at, 1), :] = 0.5 * value

    row = lax.broadcasted_iota(jnp.int32, (frame, tile_ref.shape[2]), 0)
    keep = ((row != pad - 1) | (keep_ref[0] != 0)) & ((row != pad + rows) | (keep_ref[1] != 0))

    def one_scalar(k, carry):
        index = pl.program_id(0) * block + k
        d = diff_ref[index]
        wide_ref[pl.ds(pad, rows), :] = tile_ref[k]
        wide_ref[pl.ds(pad - halo, halo), :] = below_ref[index]
        wide_ref[pl.ds(pad + rows, halo), :] = above_ref[index]
        first = advance(wide_ref[...], half0_ref[0], half0_ref[1], d)
        first = jnp.where(keep, first, 0.0)
        second = advance(first, half1_ref[0], half1_ref[1], d)
        out_ref[k] = second[pad:pad + rows]
        return carry

    lax.fori_loop(0, block, one_scalar, 0)


def body(scalars, schmidt, velocity_history, fine_src, remap_weight, snap_step):
    scal_dev, tile_rows, cells = scalars.shape
    snap_dev = velocity_history.shape[0]
    tile_count = lax.axis_size("space")
    me = lax.axis_index("space")
    anchor = me * tile_rows
    diffusivity = diffusion_scale / schmidt

    width = STEPS
    head = scalars[:, :width]
    tail = scalars[:, tile_rows - width:]
    below = lax.ppermute(tail, "space", [(i, i + 1) for i in range(tile_count - 1)])
    above = lax.ppermute(head, "space", [(i + 1, i) for i in range(tile_count - 1)])

    owners = snap_step // snap_dev
    slots = snap_step % snap_dev
    blocks = exchange(velocity_history, "scal")
    local = jnp.stack(
        [blocks[owners[step_index], slots[step_index]] for step_index in range(STEPS)]
    )
    gathered = exchange(local, "space")
    coarse = gathered.astype(jnp.float32)

    ext = tile_rows + 2 * (width - 1)
    padded_src = jnp.pad(fine_src, (1, 1))
    padded_weight = jnp.pad(remap_weight, (1, 1))
    src = lax.dynamic_slice_in_dim(padded_src, anchor, ext)
    weights = lax.dynamic_slice_in_dim(padded_weight, anchor, ext)
    keep = jnp.stack([me > 0, me < tile_count - 1]).astype(jnp.int32)

    block = 8 if scal_dev % 8 == 0 else 1
    frame = tile_rows + 16
    smem = pl.BlockSpec(memory_space=pltpu.SMEM)
    vmem = pl.BlockSpec(memory_space=pltpu.VMEM)
    tile_spec = pl.BlockSpec((block, tile_rows, cells), lambda i: (i, 0, 0))
    return pl.pallas_call(
        transport_kernel,
        grid=(scal_dev // block,),
        in_specs=[
            smem, smem, smem, smem,
            pl.BlockSpec(coarse.shape, lambda i: (0,) * coarse.ndim),
            vmem, tile_spec, vmem,
        ],
        out_specs=tile_spec,
        out_shape=jax.ShapeDtypeStruct(scalars.shape, scalars.dtype),
        scratch_shapes=[
            pltpu.VMEM((2, frame, cells), jnp.float32),
            pltpu.VMEM((2, frame, cells), jnp.float32),
            pltpu.VMEM((frame, cells), jnp.float32),
        ],
        compiler_params=pltpu.CompilerParams(dimension_semantics=("arbitrary",)),
    )(diffusivity, src, weights, keep, coarse, below, scalars, above)


def solution(mesh):
    return jax.shard_map(
        body,
        mesh=mesh,
        in_specs=(
            P("scal", "space", None),
            P("scal"),
            P("scal", None, "space", None),
            P(),
            P(),
            P(),
        ),
        out_specs=P("scal", "space", None),
        check_vma=False,
    )
```

```python
import jax
import jax.numpy as jnp
from jax import lax
from jax.experimental import pallas as pl
from jax.experimental.pallas import tpu as pltpu
from jax.sharding import PartitionSpec as P

STEPS = 2


diffusion_scale = 0.24


def exchange(value, axis):
    count = lax.axis_size(axis)
    spread = jnp.broadcast_to(value[None], (count,) + value.shape)
    return lax.all_to_all(spread, axis, 0, 0, tiled=False)


def advance(center, half_0, half_1, diffusivity):
    rows, cells = center.shape
    upper_row = pltpu.roll(center, rows - 1, 0)
    lower_row = pltpu.roll(center, 1, 0)
    east_cell = pltpu.roll(center, cells - 1, 1)
    west_cell = pltpu.roll(center, 1, 1)
    laplacian = upper_row + lower_row + east_cell + west_cell - 4.0 * center
    return (
        center
        - half_0 * (upper_row - lower_row)
        - half_1 * (east_cell - west_cell)
        + diffusivity * laplacian
    )


def transport_kernel(
    diff_ref, keep_ref, select_ref, coarse_ref, below_ref, tile_ref, above_ref,
    out_ref,
    half_ref, wide_ref,
):
    block = tile_ref.shape[0]
    rows = tile_ref.shape[1]
    halo = below_ref.shape[1]
    frame = wide_ref.shape[0]
    pad = (frame - rows) // 2

    @pl.when(pl.program_id(0) == 0)
    def _():
        wide_ref[...] = jnp.zeros_like(wide_ref)
        for step_index in range(half_ref.shape[0]):
            for comp in range(half_ref.shape[1]):
                coarse = coarse_ref[step_index, comp]
                total = None
                for part in range(select_ref.shape[0]):
                    term = jnp.dot(select_ref[part], coarse, preferred_element_type=jnp.float32)
                    total = term if total is None else total + term
                half_ref[step_index, comp] = total

    row = lax.broadcasted_iota(jnp.int32, (frame, tile_ref.shape[2]), 0)
    keep = ((row != pad - 1) | (keep_ref[0] != 0)) & ((row != pad + rows) | (keep_ref[1] != 0))

    def one_scalar(k, carry):
        index = pl.program_id(0) * block + k
        d = diff_ref[index]
        wide_ref[pl.ds(pad, rows), :] = tile_ref[k]
        wide_ref[pl.ds(pad - halo, halo), :] = below_ref[index]
        wide_ref[pl.ds(pad + rows, halo), :] = above_ref[index]
        first = advance(wide_ref[...], half_ref[0, 0], half_ref[0, 1], d)
        first = jnp.where(keep, first, 0.0)
        second = advance(first, half_ref[1, 0], half_ref[1, 1], d)
        out_ref[k] = second[pad:pad + rows]
        return carry

    lax.fori_loop(0, block, one_scalar, 0)


def body(scalars, schmidt, velocity_history, fine_src, remap_weight, snap_step):
    scal_dev, tile_rows, cells = scalars.shape
    snap_dev = velocity_history.shape[0]
    tile_count = lax.axis_size("space")
    me = lax.axis_index("space")
    anchor = me * tile_rows
    diffusivity = diffusion_scale / schmidt

    width = STEPS
    head = scalars[:, :width]
    tail = scalars[:, tile_rows - width:]
    below = lax.ppermute(tail, "space", [(i, i + 1) for i in range(tile_count - 1)])
    above = lax.ppermute(head, "space", [(i + 1, i) for i in range(tile_count - 1)])

    owners = snap_step // snap_dev
    slots = snap_step % snap_dev
    blocks = exchange(velocity_history, "scal")
    local = jnp.stack(
        [blocks[owners[step_index], slots[step_index]] for step_index in range(STEPS)]
    )
    count = lax.axis_size("space")
    spread = jnp.concatenate([local] * count, axis=2)
    coarse = lax.all_to_all(spread, "space", 2, 2, tiled=True)
    coarse_rows = coarse.shape[2]

    frame = tile_rows + 16
    pad = (frame - tile_rows) // 2
    global_row = jnp.arange(frame, dtype=jnp.int32) + anchor - pad
    valid = (global_row >= 0) & (global_row < tile_rows * tile_count)
    clipped = jnp.clip(global_row, 0, tile_rows * tile_count - 1)
    src = jnp.where(valid, fine_src[clipped], -2)
    w = jnp.where(valid, remap_weight[clipped], 0.0)
    column = lax.broadcasted_iota(jnp.int32, (frame, coarse_rows), 1)
    select = jnp.where(column == src[:, None], (0.5 * (1.0 - w))[:, None], 0.0) + jnp.where(
        column == src[:, None] + 1, (0.5 * w)[:, None], 0.0
    )
    parts = []
    rest = select
    for _ in range(3):
        piece = lax.reduce_precision(rest, exponent_bits=8, mantissa_bits=7)
        parts.append(piece.astype(jnp.bfloat16))
        rest = rest - piece
    select = jnp.stack(parts)
    keep = jnp.stack([me > 0, me < tile_count - 1]).astype(jnp.int32)

    block = 8 if scal_dev % 8 == 0 else 1
    smem = pl.BlockSpec(memory_space=pltpu.SMEM)
    vmem = pl.BlockSpec(memory_space=pltpu.VMEM)
    tile_spec = pl.BlockSpec((block, tile_rows, cells), lambda i: (i, 0, 0))
    return pl.pallas_call(
        transport_kernel,
        grid=(scal_dev // block,),
        in_specs=[
            smem, smem,
            pl.BlockSpec(select.shape, lambda i: (0,) * select.ndim),
            pl.BlockSpec(coarse.shape, lambda i: (0,) * coarse.ndim),
            vmem, tile_spec, vmem,
        ],
        out_specs=tile_spec,
        out_shape=jax.ShapeDtypeStruct(scalars.shape, scalars.dtype),
        scratch_shapes=[
            pltpu.VMEM((STEPS, 2, frame, cells), jnp.float32),
            pltpu.VMEM((frame, cells), jnp.float32),
        ],
        compiler_params=pltpu.CompilerParams(dimension_semantics=("arbitrary",)),
    )(diffusivity, keep, select, coarse, below, scalars, above)


def solution(mesh):
    return jax.shard_map(
        body,
        mesh=mesh,
        in_specs=(
            P("scal", "space", None),
            P("scal"),
            P("scal", None, "space", None),
            P(),
            P(),
            P(),
        ),
        out_specs=P("scal", "space", None),
        check_vma=False,
    )
```

```python
import jax
import jax.numpy as jnp
from jax import lax
from jax.experimental import pallas as pl
from jax.experimental.pallas import tpu as pltpu
from jax.sharding import PartitionSpec as P

STEPS = 2


diffusion_scale = 0.24


def exchange(value, axis):
    count = lax.axis_size(axis)
    spread = jnp.broadcast_to(value[None], (count,) + value.shape)
    return lax.all_to_all(spread, axis, 0, 0, tiled=False)


def advance(center, half_0, half_1, diffusivity, start, count):
    rows, cells = center.shape
    upper_row = pltpu.roll(center, rows - 1, 0)[start:start + count]
    lower_row = pltpu.roll(center, 1, 0)[start:start + count]
    east_cell = pltpu.roll(center, cells - 1, 1)[start:start + count]
    west_cell = pltpu.roll(center, 1, 1)[start:start + count]
    center = center[start:start + count]
    laplacian = upper_row + lower_row + east_cell + west_cell - 4.0 * center
    return (
        center
        - half_0[start:start + count] * (upper_row - lower_row)
        - half_1[start:start + count] * (east_cell - west_cell)
        + diffusivity * laplacian
    )


def transport_kernel(
    diff_ref, keep_ref, select_ref, coarse_ref, below_ref, tile_ref, above_ref,
    out_ref,
    half_ref, wide_ref,
):
    block = tile_ref.shape[0]
    rows = tile_ref.shape[1]
    halo = below_ref.shape[1]
    frame = wide_ref.shape[0]
    pad = (frame - rows) // 2

    @pl.when(pl.program_id(0) == 0)
    def _():
        wide_ref[...] = jnp.zeros_like(wide_ref)
        total = None
        for part in range(select_ref.shape[0]):
            term = jnp.dot(select_ref[part], coarse_ref[...], preferred_element_type=jnp.float32)
            total = term if total is None else total + term
        half_ref[...] = total

    cells = tile_ref.shape[2]

    def half(step_index, comp):
        return half_ref[:, pl.ds((step_index * 2 + comp) * cells, cells)]

    row = lax.broadcasted_iota(jnp.int32, (frame, cells), 0)
    keep = ((row != pad - 1) | (keep_ref[0] != 0)) & ((row != pad + rows) | (keep_ref[1] != 0))

    def one_scalar(k, carry):
        index = pl.program_id(0) * block + k
        d = diff_ref[index]
        wide_ref[pl.ds(pad, rows), :] = tile_ref[k]
        wide_ref[pl.ds(pad - halo, halo), :] = below_ref[index]
        wide_ref[pl.ds(pad + rows, halo), :] = above_ref[index]
        first = advance(wide_ref[...], half(0, 0), half(0, 1), d, 0, frame)
        first = jnp.where(keep, first, 0.0)
        out_ref[k] = advance(first, half(1, 0), half(1, 1), d, pad, rows)
        return carry

    lax.fori_loop(0, block, one_scalar, 0)


def body(scalars, schmidt, velocity_history, fine_src, remap_weight, snap_step):
    scal_dev, tile_rows, cells = scalars.shape
    snap_dev = velocity_history.shape[0]
    tile_count = lax.axis_size("space")
    me = lax.axis_index("space")
    anchor = me * tile_rows
    diffusivity = diffusion_scale / schmidt

    width = STEPS
    head = scalars[:, :width]
    tail = scalars[:, tile_rows - width:]
    below = lax.ppermute(tail, "space", [(i, i + 1) for i in range(tile_count - 1)])
    above = lax.ppermute(head, "space", [(i + 1, i) for i in range(tile_count - 1)])

    owners = snap_step // snap_dev
    slots = snap_step % snap_dev
    coarse_dev = velocity_history.shape[2]
    by_row = jnp.transpose(velocity_history, (2, 0, 1, 3)).reshape(coarse_dev, -1)
    slot_width = by_row.shape[1] // snap_dev
    groups = lax.axis_size("scal")
    spread = jnp.broadcast_to(by_row[None], (groups,) + by_row.shape).reshape(groups * coarse_dev, -1)
    blocks = lax.all_to_all(spread, "scal", 0, 0, tiled=True)
    blocks, below, above = lax.optimization_barrier((blocks, below, above))
    local = jnp.concatenate(
        [
            lax.dynamic_slice(
                blocks,
                (owners[step_index] * coarse_dev, slots[step_index] * slot_width),
                (coarse_dev, slot_width),
            )
            for step_index in range(STEPS)
        ],
        axis=1,
    )
    count = lax.axis_size("space")
    spread = jnp.broadcast_to(local[None], (count,) + local.shape).reshape(count * coarse_dev, -1)
    coarse = lax.all_to_all(spread, "space", 0, 0, tiled=True)
    coarse_rows = coarse.shape[0]

    frame = tile_rows + 16
    pad = (frame - tile_rows) // 2
    global_row = jnp.arange(frame, dtype=jnp.int32) + anchor - pad
    valid = (global_row >= 0) & (global_row < tile_rows * tile_count)
    clipped = jnp.clip(global_row, 0, tile_rows * tile_count - 1)
    src = jnp.where(valid, fine_src[clipped], -2)
    w = jnp.where(valid, remap_weight[clipped], 0.0)
    column = lax.broadcasted_iota(jnp.int32, (frame, coarse_rows), 1)
    select = jnp.where(column == src[:, None], (0.5 * (1.0 - w))[:, None], 0.0) + jnp.where(
        column == src[:, None] + 1, (0.5 * w)[:, None], 0.0
    )
    parts = []
    rest = select
    for _ in range(3):
        piece = lax.reduce_precision(rest, exponent_bits=8, mantissa_bits=7)
        parts.append(piece.astype(jnp.bfloat16))
        rest = rest - piece
    select = jnp.stack(parts)
    keep = jnp.stack([me > 0, me < tile_count - 1]).astype(jnp.int32)

    block = 8 if scal_dev % 8 == 0 else 1
    smem = pl.BlockSpec(memory_space=pltpu.SMEM)
    vmem = pl.BlockSpec(memory_space=pltpu.VMEM)
    tile_spec = pl.BlockSpec((block, tile_rows, cells), lambda i: (i, 0, 0))
    return pl.pallas_call(
        transport_kernel,
        grid=(scal_dev // block,),
        in_specs=[
            smem, smem,
            pl.BlockSpec(select.shape, lambda i: (0,) * select.ndim),
            pl.BlockSpec(coarse.shape, lambda i: (0,) * coarse.ndim),
            vmem, tile_spec, vmem,
        ],
        out_specs=tile_spec,
        out_shape=jax.ShapeDtypeStruct(scalars.shape, scalars.dtype),
        scratch_shapes=[
            pltpu.VMEM((frame, coarse.shape[1]), jnp.float32),
            pltpu.VMEM((frame, cells), jnp.float32),
        ],
        compiler_params=pltpu.CompilerParams(dimension_semantics=("arbitrary",)),
    )(diffusivity, keep, select, coarse, below, scalars, above)


def solution(mesh):
    return jax.shard_map(
        body,
        mesh=mesh,
        in_specs=(
            P("scal", "space", None),
            P("scal"),
            P("scal", None, "space", None),
            P(),
            P(),
            P(),
        ),
        out_specs=P("scal", "space", None),
        check_vma=False,
    )
```

```python
import jax
import jax.numpy as jnp
from jax import lax
from jax.experimental import pallas as pl
from jax.experimental.pallas import tpu as pltpu
from jax.sharding import PartitionSpec as P

STEPS = 2


diffusion_scale = 0.24


def exchange(value, axis):
    count = lax.axis_size(axis)
    spread = jnp.broadcast_to(value[None], (count,) + value.shape)
    return lax.all_to_all(spread, axis, 0, 0, tiled=False)


def advance(center, half_0, half_1, diffusivity, start, count):
    rows, cells = center.shape
    upper_row = pltpu.roll(center, rows - 1, 0)[start:start + count]
    lower_row = pltpu.roll(center, 1, 0)[start:start + count]
    east_cell = pltpu.roll(center, cells - 1, 1)[start:start + count]
    west_cell = pltpu.roll(center, 1, 1)[start:start + count]
    center = center[start:start + count]
    laplacian = upper_row + lower_row + east_cell + west_cell - 4.0 * center
    return (
        center
        - half_0[start:start + count] * (upper_row - lower_row)
        - half_1[start:start + count] * (east_cell - west_cell)
        + diffusivity * laplacian
    )


def transport_kernel(
    diff_ref, keep_ref, select_ref, coarse_ref, below_ref, tile_ref, above_ref,
    out_ref,
    half_ref, wide_ref,
):
    block = tile_ref.shape[0]
    rows = tile_ref.shape[1]
    halo = below_ref.shape[1]
    frame = wide_ref.shape[0]
    pad = (frame - rows) // 2

    @pl.when(pl.program_id(0) == 0)
    def _():
        wide_ref[...] = jnp.zeros_like(wide_ref)
        for comp in range(half_ref.shape[0]):
            total = None
            for part in range(select_ref.shape[0]):
                term = jnp.dot(
                    select_ref[part, comp], coarse_ref[...], preferred_element_type=jnp.float32
                )
                total = term if total is None else total + term
            half_ref[comp] = total

    cells = tile_ref.shape[2]

    def half(step_index, comp):
        return half_ref[comp, :, pl.ds(step_index * cells, cells)]

    row = lax.broadcasted_iota(jnp.int32, (frame, cells), 0)
    keep = ((row != pad - 1) | (keep_ref[0] != 0)) & ((row != pad + rows) | (keep_ref[1] != 0))

    def one_scalar(k, carry):
        index = pl.program_id(0) * block + k
        d = diff_ref[index]
        wide_ref[pl.ds(pad, rows), :] = tile_ref[k]
        wide_ref[pl.ds(pad - halo, halo), :] = below_ref[index]
        wide_ref[pl.ds(pad + rows, halo), :] = above_ref[index]
        first = advance(wide_ref[...], half(0, 0), half(0, 1), d, 0, frame)
        first = jnp.where(keep, first, 0.0)
        out_ref[k] = advance(first, half(1, 0), half(1, 1), d, pad, rows)
        return carry

    lax.fori_loop(0, block, one_scalar, 0)


def body(scalars, schmidt, velocity_history, fine_src, remap_weight, snap_step):
    scal_dev, tile_rows, cells = scalars.shape
    snap_dev = velocity_history.shape[0]
    tile_count = lax.axis_size("space")
    me = lax.axis_index("space")
    anchor = me * tile_rows
    diffusivity = diffusion_scale / schmidt

    width = STEPS
    head = scalars[:, :width]
    tail = scalars[:, tile_rows - width:]
    below = lax.ppermute(tail, "space", [(i, i + 1) for i in range(tile_count - 1)])
    above = lax.ppermute(head, "space", [(i + 1, i) for i in range(tile_count - 1)])

    owners = snap_step // snap_dev
    slots = snap_step % snap_dev
    slot_count, comps, coarse_dev, _ = velocity_history.shape
    by_row = jnp.transpose(velocity_history, (2, 0, 1, 3)).reshape(coarse_dev, -1)
    slot_width = by_row.shape[1] // slot_count
    groups = lax.axis_size("scal")
    spread = jnp.broadcast_to(by_row[None], (groups,) + by_row.shape).reshape(groups * coarse_dev, -1)
    blocks = lax.all_to_all(spread, "scal", 0, 0, tiled=True)
    blocks, below, above = lax.optimization_barrier((blocks, below, above))
    picked = []
    for step_index in range(STEPS):
        block = lax.dynamic_slice(
            blocks,
            (owners[step_index] * coarse_dev, slots[step_index] * slot_width),
            (coarse_dev, slot_width),
        )
        picked.append(jnp.transpose(block.reshape(coarse_dev, comps, cells), (1, 0, 2)).reshape(-1, cells))
    local = jnp.concatenate(picked, axis=1)
    height = local.shape[0]
    count = lax.axis_size("space")
    spread = jnp.broadcast_to(local[None], (count,) + local.shape).reshape(count * height, -1)
    coarse = lax.all_to_all(spread, "space", 0, 0, tiled=True)
    coarse_rows = coarse.shape[0] // comps

    frame = tile_rows + 16
    pad = (frame - tile_rows) // 2
    global_row = jnp.arange(frame, dtype=jnp.int32) + anchor - pad
    valid = (global_row >= 0) & (global_row < tile_rows * tile_count)
    clipped = jnp.clip(global_row, 0, tile_rows * tile_count - 1)
    src = jnp.where(valid, fine_src[clipped], -2)
    w = jnp.where(valid, remap_weight[clipped], 0.0)
    column = lax.broadcasted_iota(jnp.int32, (frame, coarse_rows), 1)
    select = jnp.where(column == src[:, None], (0.5 * (1.0 - w))[:, None], 0.0) + jnp.where(
        column == src[:, None] + 1, (0.5 * w)[:, None], 0.0
    )
    by_tile = select.reshape(frame, count, coarse_dev)
    select = jnp.stack(
        [
            jnp.stack([by_tile if c == comp else jnp.zeros_like(by_tile) for c in range(comps)], axis=2)
            .reshape(frame, coarse_rows * comps)
            for comp in range(comps)
        ]
    )
    parts = []
    rest = select
    for _ in range(3):
        piece = lax.reduce_precision(rest, exponent_bits=8, mantissa_bits=7)
        parts.append(piece.astype(jnp.bfloat16))
        rest = rest - piece
    select = jnp.stack(parts)
    keep = jnp.stack([me > 0, me < tile_count - 1]).astype(jnp.int32)

    block = 8 if scal_dev % 8 == 0 else 1
    smem = pl.BlockSpec(memory_space=pltpu.SMEM)
    vmem = pl.BlockSpec(memory_space=pltpu.VMEM)
    tile_spec = pl.BlockSpec((block, tile_rows, cells), lambda i: (i, 0, 0))
    return pl.pallas_call(
        transport_kernel,
        grid=(scal_dev // block,),
        in_specs=[
            smem, smem,
            pl.BlockSpec(select.shape, lambda i: (0,) * select.ndim),
            pl.BlockSpec(coarse.shape, lambda i: (0,) * coarse.ndim),
            vmem, tile_spec, vmem,
        ],
        out_specs=tile_spec,
        out_shape=jax.ShapeDtypeStruct(scalars.shape, scalars.dtype),
        scratch_shapes=[
            pltpu.VMEM((comps, frame, coarse.shape[1]), jnp.float32),
            pltpu.VMEM((frame, cells), jnp.float32),
        ],
        compiler_params=pltpu.CompilerParams(dimension_semantics=("arbitrary",)),
    )(diffusivity, keep, select, coarse, below, scalars, above)


def solution(mesh):
    return jax.shard_map(
        body,
        mesh=mesh,
        in_specs=(
            P("scal", "space", None),
            P("scal"),
            P("scal", None, "space", None),
            P(),
            P(),
            P(),
        ),
        out_specs=P("scal", "space", None),
        check_vma=False,
    )
```

```python
import jax
import jax.numpy as jnp
from jax import lax
from jax.experimental import pallas as pl
from jax.experimental.pallas import tpu as pltpu
from jax.sharding import PartitionSpec as P

STEPS = 2


diffusion_scale = 0.24


def exchange(value, axis):
    count = lax.axis_size(axis)
    spread = jnp.broadcast_to(value[None], (count,) + value.shape)
    return lax.all_to_all(spread, axis, 0, 0, tiled=False)


def advance(center, half_0, half_1, diffusivity, start, count):
    rows, cells = center.shape
    upper_row = pltpu.roll(center, rows - 1, 0)[start:start + count]
    lower_row = pltpu.roll(center, 1, 0)[start:start + count]
    east_cell = pltpu.roll(center, cells - 1, 1)[start:start + count]
    west_cell = pltpu.roll(center, 1, 1)[start:start + count]
    center = center[start:start + count]
    laplacian = upper_row + lower_row + east_cell + west_cell - 4.0 * center
    return (
        center
        - half_0[start:start + count] * (upper_row - lower_row)
        - half_1[start:start + count] * (east_cell - west_cell)
        + diffusivity * laplacian
    )


def transport_kernel(
    diff_ref, keep_ref, select_ref, coarse_ref, below_ref, tile_ref, above_ref,
    out_ref,
    half_ref, wide_ref,
):
    block = tile_ref.shape[0]
    rows = tile_ref.shape[1]
    halo = below_ref.shape[1]
    frame = wide_ref.shape[0]
    pad = (frame - rows) // 2

    @pl.when(pl.program_id(0) == 0)
    def _():
        wide_ref[...] = jnp.zeros_like(wide_ref)
        for comp in range(half_ref.shape[0]):
            total = None
            for part in range(select_ref.shape[0]):
                term = jnp.dot(
                    select_ref[part, comp], coarse_ref[...], preferred_element_type=jnp.float32
                )
                total = term if total is None else total + term
            half_ref[comp] = total

    cells = tile_ref.shape[2]

    def half(step_index, comp):
        return half_ref[comp, :, pl.ds(step_index * cells, cells)]

    edge = lax.broadcasted_iota(jnp.int32, (pad, cells), 0)
    keep_top = (edge != pad - 1) | (keep_ref[0] != 0)
    keep_bottom = (edge != 0) | (keep_ref[1] != 0)

    def one_scalar(k, carry):
        index = pl.program_id(0) * block + k
        d = diff_ref[index]
        wide_ref[pl.ds(pad, rows), :] = tile_ref[k]
        wide_ref[pl.ds(pad - halo, halo), :] = below_ref[index]
        wide_ref[pl.ds(pad + rows, halo), :] = above_ref[index]
        first = advance(wide_ref[...], half(0, 0), half(0, 1), d, 0, frame)
        first = jnp.concatenate(
            [
                jnp.where(keep_top, first[:pad], 0.0),
                first[pad:pad + rows],
                jnp.where(keep_bottom, first[pad + rows:], 0.0),
            ],
            axis=0,
        )
        out_ref[k] = advance(first, half(1, 0), half(1, 1), d, pad, rows)
        return carry

    lax.fori_loop(0, block, one_scalar, 0)


def body(scalars, schmidt, velocity_history, fine_src, remap_weight, snap_step):
    scal_dev, tile_rows, cells = scalars.shape
    snap_dev = velocity_history.shape[0]
    tile_count = lax.axis_size("space")
    me = lax.axis_index("space")
    anchor = me * tile_rows
    diffusivity = diffusion_scale / schmidt

    width = STEPS
    head = scalars[:, :width]
    tail = scalars[:, tile_rows - width:]
    below = lax.ppermute(tail, "space", [(i, i + 1) for i in range(tile_count - 1)])
    above = lax.ppermute(head, "space", [(i + 1, i) for i in range(tile_count - 1)])

    owners = snap_step // snap_dev
    slots = snap_step % snap_dev
    slot_count, comps, coarse_dev, _ = velocity_history.shape
    by_row = jnp.transpose(velocity_history, (2, 0, 1, 3)).reshape(coarse_dev, -1)
    slot_width = by_row.shape[1] // slot_count
    groups = lax.axis_size("scal")
    spread = jnp.broadcast_to(by_row[None], (groups,) + by_row.shape).reshape(groups * coarse_dev, -1)
    blocks = lax.all_to_all(spread, "scal", 0, 0, tiled=True)
    blocks, below, above = lax.optimization_barrier((blocks, below, above))
    picked = []
    for step_index in range(STEPS):
        block = lax.dynamic_slice(
            blocks,
            (owners[step_index] * coarse_dev, slots[step_index] * slot_width),
            (coarse_dev, slot_width),
        )
        picked.append(jnp.transpose(block.reshape(coarse_dev, comps, cells), (1, 0, 2)).reshape(-1, cells))
    local = jnp.concatenate(picked, axis=1)
    height = local.shape[0]
    count = lax.axis_size("space")
    spread = jnp.broadcast_to(local[None], (count,) + local.shape).reshape(count * height, -1)
    coarse = lax.all_to_all(spread, "space", 0, 0, tiled=True)
    coarse_rows = coarse.shape[0] // comps

    frame = tile_rows + 16
    pad = (frame - tile_rows) // 2
    global_row = jnp.arange(frame, dtype=jnp.int32) + anchor - pad
    valid = (global_row >= 0) & (global_row < tile_rows * tile_count)
    clipped = jnp.clip(global_row, 0, tile_rows * tile_count - 1)
    src = jnp.where(valid, fine_src[clipped], -2)
    w = jnp.where(valid, remap_weight[clipped], 0.0)
    column = lax.broadcasted_iota(jnp.int32, (frame, coarse_rows), 1)
    select = jnp.where(column == src[:, None], (0.5 * (1.0 - w))[:, None], 0.0) + jnp.where(
        column == src[:, None] + 1, (0.5 * w)[:, None], 0.0
    )
    by_tile = select.reshape(frame, count, coarse_dev)
    select = jnp.stack(
        [
            jnp.stack([by_tile if c == comp else jnp.zeros_like(by_tile) for c in range(comps)], axis=2)
            .reshape(frame, coarse_rows * comps)
            for comp in range(comps)
        ]
    )
    parts = []
    rest = select
    for _ in range(3):
        piece = lax.reduce_precision(rest, exponent_bits=8, mantissa_bits=7)
        parts.append(piece.astype(jnp.bfloat16))
        rest = rest - piece
    select = jnp.stack(parts)
    keep = jnp.stack([me > 0, me < tile_count - 1]).astype(jnp.int32)

    block = 16 if scal_dev % 16 == 0 else 1
    smem = pl.BlockSpec(memory_space=pltpu.SMEM)
    vmem = pl.BlockSpec(memory_space=pltpu.VMEM)
    tile_spec = pl.BlockSpec((block, tile_rows, cells), lambda i: (i, 0, 0))
    return pl.pallas_call(
        transport_kernel,
        grid=(scal_dev // block,),
        in_specs=[
            smem, smem,
            pl.BlockSpec(select.shape, lambda i: (0,) * select.ndim),
            pl.BlockSpec(coarse.shape, lambda i: (0,) * coarse.ndim),
            vmem, tile_spec, vmem,
        ],
        out_specs=tile_spec,
        out_shape=jax.ShapeDtypeStruct(scalars.shape, scalars.dtype),
        scratch_shapes=[
            pltpu.VMEM((comps, frame, coarse.shape[1]), jnp.float32),
            pltpu.VMEM((frame, cells), jnp.float32),
        ],
        compiler_params=pltpu.CompilerParams(dimension_semantics=("arbitrary",)),
    )(diffusivity, keep, select, coarse, below, scalars, above)


def solution(mesh):
    return jax.shard_map(
        body,
        mesh=mesh,
        in_specs=(
            P("scal", "space", None),
            P("scal"),
            P("scal", None, "space", None),
            P(),
            P(),
            P(),
        ),
        out_specs=P("scal", "space", None),
        check_vma=False,
    )
```

```python
import jax
import jax.numpy as jnp
from jax import lax
from jax.experimental import pallas as pl
from jax.experimental.pallas import tpu as pltpu
from jax.sharding import PartitionSpec as P

STEPS = 2


diffusion_scale = 0.24


def exchange(value, axis):
    count = lax.axis_size(axis)
    spread = jnp.broadcast_to(value[None], (count,) + value.shape)
    return lax.all_to_all(spread, axis, 0, 0, tiled=False)


def advance(center, half_0, half_1, diffusivity, start, count):
    rows, cells = center.shape
    upper_row = pltpu.roll(center, rows - 1, 0)[start:start + count]
    lower_row = pltpu.roll(center, 1, 0)[start:start + count]
    east_cell = pltpu.roll(center, cells - 1, 1)[start:start + count]
    west_cell = pltpu.roll(center, 1, 1)[start:start + count]
    center = center[start:start + count]
    laplacian = upper_row + lower_row + east_cell + west_cell - 4.0 * center
    return (
        center
        - half_0[start:start + count] * (upper_row - lower_row)
        - half_1[start:start + count] * (east_cell - west_cell)
        + diffusivity * laplacian
    )


def transport_kernel(
    diff_ref, keep_ref, select_ref, coarse_ref, below_ref, tile_ref, above_ref,
    out_ref,
    half_ref, wide_ref,
):
    block = tile_ref.shape[0]
    rows = tile_ref.shape[1]
    halo = below_ref.shape[1]
    frame = wide_ref.shape[0]
    pad = (frame - rows) // 2

    @pl.when(pl.program_id(0) == 0)
    def _():
        wide_ref[...] = jnp.zeros_like(wide_ref)
        for comp in range(half_ref.shape[0]):
            total = None
            for part in range(select_ref.shape[0]):
                term = jnp.dot(
                    select_ref[part, comp], coarse_ref[...], preferred_element_type=jnp.float32
                )
                total = term if total is None else total + term
            half_ref[comp] = total

    cells = tile_ref.shape[2]

    def half(step_index, comp):
        return half_ref[comp, :, pl.ds(step_index * cells, cells)]

    edge = lax.broadcasted_iota(jnp.int32, (pad, cells), 0)
    keep_top = (edge != pad - 1) | (keep_ref[0] != 0)
    keep_bottom = (edge != 0) | (keep_ref[1] != 0)

    def one_scalar(k, carry):
        index = pl.program_id(0) * block + k
        d = diff_ref[index]
        wide_ref[pl.ds(pad, rows), :] = tile_ref[k]
        wide_ref[pl.ds(pad - halo, halo), :] = below_ref[index]
        wide_ref[pl.ds(pad + rows, halo), :] = above_ref[index]
        first = advance(wide_ref[...], half(0, 0), half(0, 1), d, 0, frame)
        first = jnp.concatenate(
            [
                jnp.where(keep_top, first[:pad], 0.0),
                first[pad:pad + rows],
                jnp.where(keep_bottom, first[pad + rows:], 0.0),
            ],
            axis=0,
        )
        out_ref[k] = advance(first, half(1, 0), half(1, 1), d, pad, rows)
        return carry

    lax.fori_loop(0, block, one_scalar, 0)


def body(scalars, schmidt, velocity_history, fine_src, remap_weight, snap_step):
    scal_dev, tile_rows, cells = scalars.shape
    snap_dev = velocity_history.shape[0]
    tile_count = lax.axis_size("space")
    me = lax.axis_index("space")
    anchor = me * tile_rows
    diffusivity = diffusion_scale / schmidt

    width = STEPS
    head = scalars[:, :width]
    tail = scalars[:, tile_rows - width:]
    below = lax.ppermute(tail, "space", [(i, i + 1) for i in range(tile_count - 1)])
    above = lax.ppermute(head, "space", [(i + 1, i) for i in range(tile_count - 1)])

    owners = snap_step // snap_dev
    slots = snap_step % snap_dev
    slot_count, comps, coarse_dev, _ = velocity_history.shape
    by_row = velocity_history.reshape(slot_count * comps * coarse_dev, cells)
    groups = lax.axis_size("scal")
    spread = jnp.broadcast_to(by_row[None], (groups,) + by_row.shape).reshape(-1, cells)
    blocks = lax.all_to_all(spread, "scal", 0, 0, tiled=True)
    blocks, below, above = lax.optimization_barrier((blocks, below, above))
    height = comps * coarse_dev
    local = jnp.concatenate(
        [
            lax.dynamic_slice_in_dim(
                blocks, (owners[step_index] * slot_count + slots[step_index]) * height, height
            )
            for step_index in range(STEPS)
        ],
        axis=1,
    )
    count = lax.axis_size("space")
    spread = jnp.broadcast_to(local[None], (count,) + local.shape).reshape(count * height, -1)
    coarse = lax.all_to_all(spread, "space", 0, 0, tiled=True)
    coarse_rows = coarse.shape[0] // comps

    frame = tile_rows + 16
    pad = (frame - tile_rows) // 2
    global_row = jnp.arange(frame, dtype=jnp.int32) + anchor - pad
    valid = (global_row >= 0) & (global_row < tile_rows * tile_count)
    clipped = jnp.clip(global_row, 0, tile_rows * tile_count - 1)
    src = jnp.where(valid, fine_src[clipped], -2)
    w = jnp.where(valid, remap_weight[clipped], 0.0)
    column = lax.broadcasted_iota(jnp.int32, (frame, coarse_rows), 1)
    select = jnp.where(column == src[:, None], (0.5 * (1.0 - w))[:, None], 0.0) + jnp.where(
        column == src[:, None] + 1, (0.5 * w)[:, None], 0.0
    )
    by_tile = select.reshape(frame, count, coarse_dev)
    select = jnp.stack(
        [
            jnp.stack([by_tile if c == comp else jnp.zeros_like(by_tile) for c in range(comps)], axis=2)
            .reshape(frame, coarse_rows * comps)
            for comp in range(comps)
        ]
    )
    parts = []
    rest = select
    for _ in range(3):
        piece = lax.reduce_precision(rest, exponent_bits=8, mantissa_bits=7)
        parts.append(piece.astype(jnp.bfloat16))
        rest = rest - piece
    select = jnp.stack(parts)
    keep = jnp.stack([me > 0, me < tile_count - 1]).astype(jnp.int32)

    block = 16 if scal_dev % 16 == 0 else 1
    smem = pl.BlockSpec(memory_space=pltpu.SMEM)
    vmem = pl.BlockSpec(memory_space=pltpu.VMEM)
    tile_spec = pl.BlockSpec((block, tile_rows, cells), lambda i: (i, 0, 0))
    return pl.pallas_call(
        transport_kernel,
        grid=(scal_dev // block,),
        in_specs=[
            smem, smem,
            pl.BlockSpec(select.shape, lambda i: (0,) * select.ndim),
            vmem,
            vmem, tile_spec, vmem,
        ],
        out_specs=tile_spec,
        out_shape=jax.ShapeDtypeStruct(scalars.shape, scalars.dtype),
        scratch_shapes=[
            pltpu.VMEM((comps, frame, coarse.shape[1]), jnp.float32),
            pltpu.VMEM((frame, cells), jnp.float32),
        ],
        compiler_params=pltpu.CompilerParams(dimension_semantics=("arbitrary",)),
    )(diffusivity, keep, select, coarse, below, scalars, above)


def solution(mesh):
    return jax.shard_map(
        body,
        mesh=mesh,
        in_specs=(
            P("scal", "space", None),
            P("scal"),
            P("scal", None, "space", None),
            P(),
            P(),
            P(),
        ),
        out_specs=P("scal", "space", None),
        check_vma=False,
    )
```

```python
import jax
import jax.numpy as jnp
from jax import lax
from jax.experimental import pallas as pl
from jax.experimental.pallas import tpu as pltpu
from jax.sharding import PartitionSpec as P

STEPS = 2


diffusion_scale = 0.24


def exchange(value, axis):
    count = lax.axis_size(axis)
    spread = jnp.broadcast_to(value[None], (count,) + value.shape)
    return lax.all_to_all(spread, axis, 0, 0, tiled=False)


def advance(center, half_0, half_1, diffusivity, start, count):
    rows, cells = center.shape
    upper_row = pltpu.roll(center, rows - 1, 0)[start:start + count]
    lower_row = pltpu.roll(center, 1, 0)[start:start + count]
    east_cell = pltpu.roll(center, cells - 1, 1)[start:start + count]
    west_cell = pltpu.roll(center, 1, 1)[start:start + count]
    center = center[start:start + count]
    laplacian = upper_row + lower_row + east_cell + west_cell - 4.0 * center
    return (
        center
        - half_0[start:start + count] * (upper_row - lower_row)
        - half_1[start:start + count] * (east_cell - west_cell)
        + diffusivity * laplacian
    )


def transport_kernel(
    diff_ref, keep_ref, select_ref, coarse_ref, below_ref, tile_ref, above_ref,
    out_ref,
    half_ref, wide_ref,
):
    block = tile_ref.shape[0]
    rows = tile_ref.shape[1]
    halo = below_ref.shape[1]
    frame = wide_ref.shape[0]
    pad = (frame - rows) // 2

    @pl.when(pl.program_id(0) == 0)
    def _():
        wide_ref[...] = jnp.zeros_like(wide_ref)
        for comp in range(half_ref.shape[0]):
            total = None
            for part in range(select_ref.shape[0]):
                term = jnp.dot(
                    select_ref[part, comp], coarse_ref[...], preferred_element_type=jnp.float32
                )
                total = term if total is None else total + term
            half_ref[comp] = total

    cells = tile_ref.shape[2]

    def half(step_index, comp):
        return half_ref[comp, :, pl.ds(step_index * cells, cells)]

    edge = lax.broadcasted_iota(jnp.int32, (pad, cells), 0)
    keep_top = (edge != pad - 1) | (keep_ref[0] != 0)
    keep_bottom = (edge != 0) | (keep_ref[1] != 0)

    def one_scalar(k, carry):
        index = pl.program_id(0) * block + k
        d = diff_ref[index]
        wide_ref[pl.ds(pad, rows), :] = tile_ref[k]
        wide_ref[pl.ds(pad - halo, halo), :] = below_ref[index]
        wide_ref[pl.ds(pad + rows, halo), :] = above_ref[index]
        first = advance(wide_ref[...], half(0, 0), half(0, 1), d, 0, frame)
        first = jnp.concatenate(
            [
                jnp.where(keep_top, first[:pad], 0.0),
                first[pad:pad + rows],
                jnp.where(keep_bottom, first[pad + rows:], 0.0),
            ],
            axis=0,
        )
        out_ref[k] = advance(first, half(1, 0), half(1, 1), d, pad, rows)
        return carry

    lax.fori_loop(0, block, one_scalar, 0)


def body(scalars, schmidt, velocity_history, fine_src, remap_weight, snap_step):
    scal_dev, tile_rows, cells = scalars.shape
    slot_count, comps, coarse_dev, _ = velocity_history.shape
    size = lambda name: lax.axis_size(name)
    tile_count = size("zl") * size("x")
    me = lax.axis_index("zl") * size("x") + lax.axis_index("x")
    anchor = me * tile_rows
    diffusivity = diffusion_scale / schmidt

    width = STEPS
    head = scalars[:, :width]
    tail = scalars[:, tile_rows - width:]
    below = lax.ppermute(tail, SPACE, [(i, i + 1) for i in range(tile_count - 1)])
    above = lax.ppermute(head, SPACE, [(i + 1, i) for i in range(tile_count - 1)])

    owners = snap_step // slot_count
    slots = snap_step % slot_count
    owner_c = owners % size("c")
    owner_zh = (owners // size("c")) % size("zh")
    owner_y = owners // (size("c") * size("zh"))
    height = comps * coarse_dev

    def spread(block, count):
        return jnp.broadcast_to(block[None], (count,) + block.shape).reshape(-1, block.shape[1])

    by_row = velocity_history.reshape(slot_count * height, cells)
    peers = size("y") * size("c")
    first = lax.all_to_all(spread(by_row, peers), ("y", "c"), 0, 0, tiled=True)
    first, below, above = lax.optimization_barrier((first, below, above))
    local = jnp.concatenate(
        [
            lax.dynamic_slice_in_dim(
                first,
                ((owner_y[t] * size("c") + owner_c[t]) * slot_count + slots[t]) * height,
                height,
            )
            for t in range(STEPS)
        ],
        axis=1,
    )

    ring = size("zh") * size("zl")
    second = lax.all_to_all(spread(local, ring), ("zh", "zl"), 0, 0, tiled=True)
    half_rows = size("zl") * height
    column = jnp.concatenate(
        [
            lax.dynamic_slice(second, (owner_zh[t] * half_rows, t * cells), (half_rows, cells))
            for t in range(STEPS)
        ],
        axis=1,
    )

    coarse = lax.all_to_all(spread(column, size("x")), "x", 0, 0, tiled=True)
    coarse_rows = tile_count * coarse_dev

    frame = tile_rows + 16
    pad = (frame - tile_rows) // 2
    global_row = jnp.arange(frame, dtype=jnp.int32) + anchor - pad
    valid = (global_row >= 0) & (global_row < tile_rows * tile_count)
    clipped = jnp.clip(global_row, 0, tile_rows * tile_count - 1)
    src = jnp.where(valid, fine_src[clipped], -2)
    w = jnp.where(valid, remap_weight[clipped], 0.0)
    column_index = lax.broadcasted_iota(jnp.int32, (frame, coarse_rows), 1)
    select = jnp.where(column_index == src[:, None], (0.5 * (1.0 - w))[:, None], 0.0) + jnp.where(
        column_index == src[:, None] + 1, (0.5 * w)[:, None], 0.0
    )
    by_tile = select.reshape(frame, size("zl"), size("x"), coarse_dev).transpose(0, 2, 1, 3)
    select = jnp.stack(
        [
            jnp.stack(
                [by_tile if c == comp else jnp.zeros_like(by_tile) for c in range(comps)], axis=3
            ).reshape(frame, coarse_rows * comps)
            for comp in range(comps)
        ]
    )
    parts = []
    rest = select
    for _ in range(3):
        piece = lax.reduce_precision(rest, exponent_bits=8, mantissa_bits=7)
        parts.append(piece.astype(jnp.bfloat16))
        rest = rest - piece
    select = jnp.stack(parts)
    keep = jnp.stack([me > 0, me < tile_count - 1]).astype(jnp.int32)

    block = 16 if scal_dev % 16 == 0 else 1
    smem = pl.BlockSpec(memory_space=pltpu.SMEM)
    vmem = pl.BlockSpec(memory_space=pltpu.VMEM)
    tile_spec = pl.BlockSpec((block, tile_rows, cells), lambda i: (i, 0, 0))
    return pl.pallas_call(
        transport_kernel,
        grid=(scal_dev // block,),
        in_specs=[
            smem, smem,
            pl.BlockSpec(select.shape, lambda i: (0,) * select.ndim),
            vmem,
            vmem, tile_spec, vmem,
        ],
        out_specs=tile_spec,
        out_shape=jax.ShapeDtypeStruct(scalars.shape, scalars.dtype),
        scratch_shapes=[
            pltpu.VMEM((comps, frame, coarse.shape[1]), jnp.float32),
            pltpu.VMEM((frame, cells), jnp.float32),
        ],
        compiler_params=pltpu.CompilerParams(dimension_semantics=("arbitrary",)),
    )(diffusivity, keep, select, coarse, below, scalars, above)


SPACE = ("zl", "x")
SCAL = ("y", "zh", "c")


def solution(mesh):
    space, scal = mesh.shape["space"], mesh.shape["scal"]
    devices = mesh.devices.reshape(space // 4, 4, scal // 4, 2, 2)
    named = jax.sharding.Mesh(devices, SPACE + SCAL)
    return jax.shard_map(
        body,
        mesh=named,
        in_specs=(
            P(SCAL, SPACE, None),
            P(SCAL),
            P(SCAL, None, SPACE, None),
            P(),
            P(),
            P(),
        ),
        out_specs=P(SCAL, SPACE, None),
        check_vma=False,
    )
```

```python
import jax
import jax.numpy as jnp
from jax import lax
from jax.experimental import pallas as pl
from jax.experimental.pallas import tpu as pltpu
from jax.sharding import PartitionSpec as P

STEPS = 2


diffusion_scale = 0.24


def exchange(value, axis):
    count = lax.axis_size(axis)
    spread = jnp.broadcast_to(value[None], (count,) + value.shape)
    return lax.all_to_all(spread, axis, 0, 0, tiled=False)


def advance(center, half_0, half_1, diffusivity, start, count):
    rows, cells = center.shape
    upper_row = pltpu.roll(center, rows - 1, 0)[start:start + count]
    lower_row = pltpu.roll(center, 1, 0)[start:start + count]
    east_cell = pltpu.roll(center, cells - 1, 1)[start:start + count]
    west_cell = pltpu.roll(center, 1, 1)[start:start + count]
    center = center[start:start + count]
    laplacian = upper_row + lower_row + east_cell + west_cell - 4.0 * center
    return (
        center
        - half_0[start:start + count] * (upper_row - lower_row)
        - half_1[start:start + count] * (east_cell - west_cell)
        + diffusivity * laplacian
    )


def transport_kernel(
    diff_ref, keep_ref, select_ref, coarse_ref, below_ref, tile_ref, above_ref,
    out_ref,
    half_ref, wide_ref,
):
    block = tile_ref.shape[0]
    rows = tile_ref.shape[1]
    halo = below_ref.shape[1]
    frame = wide_ref.shape[0]
    pad = (frame - rows) // 2

    @pl.when(pl.program_id(0) == 0)
    def _():
        wide_ref[...] = jnp.zeros_like(wide_ref)
        for comp in range(half_ref.shape[0]):
            total = None
            for part in range(select_ref.shape[0]):
                term = jnp.dot(
                    select_ref[part, comp], coarse_ref[...], preferred_element_type=jnp.float32
                )
                total = term if total is None else total + term
            half_ref[comp] = total

    cells = tile_ref.shape[2]

    def half(step_index, comp):
        return half_ref[comp, :, pl.ds(step_index * cells, cells)]

    edge = lax.broadcasted_iota(jnp.int32, (pad, cells), 0)
    keep_top = (edge != pad - 1) | (keep_ref[0] != 0)
    keep_bottom = (edge != 0) | (keep_ref[1] != 0)

    def one_scalar(k, carry):
        index = pl.program_id(0) * block + k
        d = diff_ref[index]
        wide_ref[pl.ds(pad, rows), :] = tile_ref[k]
        wide_ref[pl.ds(pad - halo, halo), :] = below_ref[index]
        wide_ref[pl.ds(pad + rows, halo), :] = above_ref[index]
        first = advance(wide_ref[...], half(0, 0), half(0, 1), d, 0, frame)
        first = jnp.concatenate(
            [
                jnp.where(keep_top, first[:pad], 0.0),
                first[pad:pad + rows],
                jnp.where(keep_bottom, first[pad + rows:], 0.0),
            ],
            axis=0,
        )
        out_ref[k] = advance(first, half(1, 0), half(1, 1), d, pad, rows)
        return carry

    lax.fori_loop(0, block, one_scalar, 0)


def body(scalars, schmidt, velocity_history, fine_src, remap_weight, snap_step):
    scal_dev, tile_rows, cells = scalars.shape
    slot_count, comps, coarse_dev, _ = velocity_history.shape
    size = lambda name: lax.axis_size(name)
    tile_count = size("zl") * size("x")
    me = lax.axis_index("zl") * size("x") + lax.axis_index("x")
    anchor = me * tile_rows
    diffusivity = diffusion_scale / schmidt

    width = STEPS
    head = scalars[:, :width]
    tail = scalars[:, tile_rows - width:]

    owners = snap_step // slot_count
    slots = snap_step % slot_count
    owner_c = owners % size("c")
    owner_zh = (owners // size("c")) % size("zh")
    owner_y = owners // (size("c") * size("zh"))
    height = comps * coarse_dev

    def spread(block, count):
        return jnp.broadcast_to(block[None], (count,) + block.shape).reshape(-1, block.shape[1])

    by_row = velocity_history.reshape(slot_count * height, cells)
    peers = size("y") * size("c")
    first = lax.all_to_all(spread(by_row, peers), ("y", "c"), 0, 0, tiled=True)
    first, head, tail, fine_src, remap_weight = lax.optimization_barrier(
        (first, head, tail, fine_src, remap_weight)
    )
    below = lax.ppermute(tail, SPACE, [(i, i + 1) for i in range(tile_count - 1)])
    above = lax.ppermute(head, SPACE, [(i + 1, i) for i in range(tile_count - 1)])
    local = jnp.concatenate(
        [
            lax.dynamic_slice_in_dim(
                first,
                ((owner_y[t] * size("c") + owner_c[t]) * slot_count + slots[t]) * height,
                height,
            )
            for t in range(STEPS)
        ],
        axis=1,
    )

    ring = size("zh") * size("zl")
    second = lax.all_to_all(spread(local, ring), ("zh", "zl"), 0, 0, tiled=True)
    half_rows = size("zl") * height
    column = jnp.concatenate(
        [
            lax.dynamic_slice(second, (owner_zh[t] * half_rows, t * cells), (half_rows, cells))
            for t in range(STEPS)
        ],
        axis=1,
    )

    coarse = lax.all_to_all(spread(column, size("x")), "x", 0, 0, tiled=True)
    coarse_rows = tile_count * coarse_dev

    frame = tile_rows + 16
    pad = (frame - tile_rows) // 2
    global_row = jnp.arange(frame, dtype=jnp.int32) + anchor - pad
    valid = (global_row >= 0) & (global_row < tile_rows * tile_count)
    clipped = jnp.clip(global_row, 0, tile_rows * tile_count - 1)
    src = jnp.where(valid, fine_src[clipped], -2)
    w = jnp.where(valid, remap_weight[clipped], 0.0)
    column_index = lax.broadcasted_iota(jnp.int32, (frame, coarse_rows), 1)
    select = jnp.where(column_index == src[:, None], (0.5 * (1.0 - w))[:, None], 0.0) + jnp.where(
        column_index == src[:, None] + 1, (0.5 * w)[:, None], 0.0
    )
    by_tile = select.reshape(frame, size("zl"), size("x"), coarse_dev).transpose(0, 2, 1, 3)
    select = jnp.stack(
        [
            jnp.stack(
                [by_tile if c == comp else jnp.zeros_like(by_tile) for c in range(comps)], axis=3
            ).reshape(frame, coarse_rows * comps)
            for comp in range(comps)
        ]
    )
    parts = []
    rest = select
    for _ in range(3):
        piece = lax.reduce_precision(rest, exponent_bits=8, mantissa_bits=7)
        parts.append(piece.astype(jnp.bfloat16))
        rest = rest - piece
    select = jnp.stack(parts)
    keep = jnp.stack([me > 0, me < tile_count - 1]).astype(jnp.int32)

    block = 16 if scal_dev % 16 == 0 else 1
    smem = pl.BlockSpec(memory_space=pltpu.SMEM)
    vmem = pl.BlockSpec(memory_space=pltpu.VMEM)
    tile_spec = pl.BlockSpec((block, tile_rows, cells), lambda i: (i, 0, 0))
    return pl.pallas_call(
        transport_kernel,
        grid=(scal_dev // block,),
        in_specs=[
            smem, smem,
            pl.BlockSpec(select.shape, lambda i: (0,) * select.ndim),
            vmem,
            vmem, tile_spec, vmem,
        ],
        out_specs=tile_spec,
        out_shape=jax.ShapeDtypeStruct(scalars.shape, scalars.dtype),
        scratch_shapes=[
            pltpu.VMEM((comps, frame, coarse.shape[1]), jnp.float32),
            pltpu.VMEM((frame, cells), jnp.float32),
        ],
        compiler_params=pltpu.CompilerParams(dimension_semantics=("arbitrary",)),
    )(diffusivity, keep, select, coarse, below, scalars, above)


SPACE = ("zl", "x")
SCAL = ("y", "zh", "c")


def solution(mesh):
    space, scal = mesh.shape["space"], mesh.shape["scal"]
    devices = mesh.devices.reshape(space // 4, 4, scal // 4, 2, 2)
    named = jax.sharding.Mesh(devices, SPACE + SCAL)
    return jax.shard_map(
        body,
        mesh=named,
        in_specs=(
            P(SCAL, SPACE, None),
            P(SCAL),
            P(SCAL, None, SPACE, None),
            P(),
            P(),
            P(),
        ),
        out_specs=P(SCAL, SPACE, None),
        check_vma=False,
    )
```

```python
import jax
import jax.numpy as jnp
from jax import lax
from jax.experimental import pallas as pl
from jax.experimental.pallas import tpu as pltpu
from jax.sharding import PartitionSpec as P

STEPS = 2


diffusion_scale = 0.24


def advance(center, half_0, half_1, diffusivity, start, count):
    rows, cells = center.shape
    upper_row = pltpu.roll(center, rows - 1, 0)[start:start + count]
    lower_row = pltpu.roll(center, 1, 0)[start:start + count]
    east_cell = pltpu.roll(center, cells - 1, 1)[start:start + count]
    west_cell = pltpu.roll(center, 1, 1)[start:start + count]
    center = center[start:start + count]
    laplacian = upper_row + lower_row + east_cell + west_cell - 4.0 * center
    return (
        center
        - half_0[start:start + count] * (upper_row - lower_row)
        - half_1[start:start + count] * (east_cell - west_cell)
        + diffusivity * laplacian
    )


def transport_kernel(
    diff_ref, keep_ref, select_ref, coarse_ref, below_ref, tile_ref, above_ref,
    out_ref,
    half_ref, wide_ref,
):
    block = tile_ref.shape[0]
    rows = tile_ref.shape[1]
    halo = below_ref.shape[1]
    frame = wide_ref.shape[0]
    pad = (frame - rows) // 2

    @pl.when(pl.program_id(0) == 0)
    def _():
        wide_ref[...] = jnp.zeros_like(wide_ref)
        for comp in range(half_ref.shape[0]):
            total = None
            for part in range(select_ref.shape[0]):
                term = jnp.concatenate(
                    [
                        jnp.dot(
                            select_ref[part, comp],
                            coarse_ref[:, step_index].reshape(-1, coarse_ref.shape[3]),
                            preferred_element_type=jnp.float32,
                        )
                        for step_index in range(coarse_ref.shape[1])
                    ],
                    axis=1,
                )
                total = term if total is None else total + term
            half_ref[comp] = total

    cells = tile_ref.shape[2]

    def half(step_index, comp):
        return half_ref[comp, :, pl.ds(step_index * cells, cells)]

    edge = lax.broadcasted_iota(jnp.int32, (pad, cells), 0)
    keep_top = (edge != pad - 1) | (keep_ref[0] != 0)
    keep_bottom = (edge != 0) | (keep_ref[1] != 0)

    def one_scalar(k, carry):
        index = pl.program_id(0) * block + k
        d = diff_ref[index]
        wide_ref[pl.ds(pad, rows), :] = tile_ref[k]
        wide_ref[pl.ds(pad - halo, halo), :] = below_ref[index]
        wide_ref[pl.ds(pad + rows, halo), :] = above_ref[index]
        first = advance(wide_ref[...], half(0, 0), half(0, 1), d, 0, frame)
        first = jnp.concatenate(
            [
                jnp.where(keep_top, first[:pad], 0.0),
                first[pad:pad + rows],
                jnp.where(keep_bottom, first[pad + rows:], 0.0),
            ],
            axis=0,
        )
        out_ref[k] = advance(first, half(1, 0), half(1, 1), d, pad, rows)
        return carry

    lax.fori_loop(0, block, one_scalar, 0)


def body(scalars, schmidt, velocity_history, fine_src, remap_weight, snap_step):
    scal_dev, tile_rows, cells = scalars.shape
    slot_count, comps, coarse_dev, _ = velocity_history.shape
    size = lambda name: lax.axis_size(name)
    tile_count = size("zl") * size("x")
    me = lax.axis_index("zl") * size("x") + lax.axis_index("x")
    anchor = me * tile_rows
    diffusivity = diffusion_scale / schmidt

    width = STEPS
    head = scalars[:, :width]
    tail = scalars[:, tile_rows - width:]

    owners = snap_step // slot_count
    slots = snap_step % slot_count
    owner_c = owners % size("c")
    owner_zh = (owners // size("c")) % size("zh")
    owner_y = owners // (size("c") * size("zh"))
    height = comps * coarse_dev

    def spread(block, count):
        return jnp.broadcast_to(block[None], (count,) + block.shape).reshape(-1, block.shape[1])

    by_row = velocity_history.reshape(slot_count * height, cells)
    peers = size("y") * size("c")
    first = lax.all_to_all(spread(by_row, peers), ("y", "c"), 0, 0, tiled=True)
    first, head, tail, fine_src, remap_weight = lax.optimization_barrier(
        (first, head, tail, fine_src, remap_weight)
    )
    below = lax.ppermute(tail, SPACE, [(i, i + 1) for i in range(tile_count - 1)])
    above = lax.ppermute(head, SPACE, [(i + 1, i) for i in range(tile_count - 1)])
    local = jnp.concatenate(
        [
            lax.dynamic_slice_in_dim(
                first,
                ((owner_y[t] * size("c") + owner_c[t]) * slot_count + slots[t]) * height,
                height,
            )
            for t in range(STEPS)
        ],
        axis=1,
    )

    core = lax.axis_index("c")
    mine = lax.dynamic_slice_in_dim(local, core * cells, cells, axis=1)
    core_zh = lax.dynamic_index_in_dim(owner_zh, core, keepdims=False)

    ring = size("zh") * size("zl")
    second = lax.all_to_all(spread(mine, ring), ("zh", "zl"), 0, 0, tiled=True)
    half_rows = size("zl") * height
    column = lax.dynamic_slice_in_dim(second, core_zh * half_rows, half_rows)

    coarse = lax.all_to_all(spread(column, size("x") * size("c")), ("x", "c"), 0, 0, tiled=True)
    coarse = coarse.reshape(size("x"), size("c"), half_rows, cells)
    coarse_rows = tile_count * coarse_dev

    frame = tile_rows + 16
    pad = (frame - tile_rows) // 2
    global_row = jnp.arange(frame, dtype=jnp.int32) + anchor - pad
    valid = (global_row >= 0) & (global_row < tile_rows * tile_count)
    clipped = jnp.clip(global_row, 0, tile_rows * tile_count - 1)
    src = jnp.where(valid, fine_src[clipped], -2)
    w = jnp.where(valid, remap_weight[clipped], 0.0)
    column_index = lax.broadcasted_iota(jnp.int32, (frame, coarse_rows), 1)
    select = jnp.where(column_index == src[:, None], (0.5 * (1.0 - w))[:, None], 0.0) + jnp.where(
        column_index == src[:, None] + 1, (0.5 * w)[:, None], 0.0
    )
    by_tile = select.reshape(frame, size("zl"), size("x"), coarse_dev).transpose(0, 2, 1, 3)
    select = jnp.stack(
        [
            jnp.stack(
                [by_tile if c == comp else jnp.zeros_like(by_tile) for c in range(comps)], axis=3
            ).reshape(frame, coarse_rows * comps)
            for comp in range(comps)
        ]
    )
    parts = []
    rest = select
    for _ in range(3):
        piece = lax.reduce_precision(rest, exponent_bits=8, mantissa_bits=7)
        parts.append(piece.astype(jnp.bfloat16))
        rest = rest - piece
    select = jnp.stack(parts)
    keep = jnp.stack([me > 0, me < tile_count - 1]).astype(jnp.int32)

    block = 16 if scal_dev % 16 == 0 else 1
    smem = pl.BlockSpec(memory_space=pltpu.SMEM)
    vmem = pl.BlockSpec(memory_space=pltpu.VMEM)
    tile_spec = pl.BlockSpec((block, tile_rows, cells), lambda i: (i, 0, 0))
    return pl.pallas_call(
        transport_kernel,
        grid=(scal_dev // block,),
        in_specs=[
            smem, smem,
            pl.BlockSpec(select.shape, lambda i: (0,) * select.ndim),
            vmem,
            vmem, tile_spec, vmem,
        ],
        out_specs=tile_spec,
        out_shape=jax.ShapeDtypeStruct(scalars.shape, scalars.dtype),
        scratch_shapes=[
            pltpu.VMEM((comps, frame, STEPS * cells), jnp.float32),
            pltpu.VMEM((frame, cells), jnp.float32),
        ],
        compiler_params=pltpu.CompilerParams(dimension_semantics=("arbitrary",)),
    )(diffusivity, keep, select, coarse, below, scalars, above)


SPACE = ("zl", "x")
SCAL = ("y", "zh", "c")


def solution(mesh):
    space, scal = mesh.shape["space"], mesh.shape["scal"]
    devices = mesh.devices.reshape(space // 4, 4, scal // 4, 2, 2)
    named = jax.sharding.Mesh(devices, SPACE + SCAL)
    return jax.shard_map(
        body,
        mesh=named,
        in_specs=(
            P(SCAL, SPACE, None),
            P(SCAL),
            P(SCAL, None, SPACE, None),
            P(),
            P(),
            P(),
        ),
        out_specs=P(SCAL, SPACE, None),
        check_vma=False,
    )
```

```python
import jax
import jax.numpy as jnp
from jax import lax
from jax.experimental import pallas as pl
from jax.experimental.pallas import tpu as pltpu
from jax.sharding import PartitionSpec as P

STEPS = 2


diffusion_scale = 0.24


def advance(center, half_0, half_1, diffusivity, start, count):
    rows, cells = center.shape
    upper_row = pltpu.roll(center, rows - 1, 0)[start:start + count]
    lower_row = pltpu.roll(center, 1, 0)[start:start + count]
    east_cell = pltpu.roll(center, cells - 1, 1)[start:start + count]
    west_cell = pltpu.roll(center, 1, 1)[start:start + count]
    center = center[start:start + count]
    laplacian = upper_row + lower_row + east_cell + west_cell - 4.0 * center
    return (
        center
        - half_0[start:start + count] * (upper_row - lower_row)
        - half_1[start:start + count] * (east_cell - west_cell)
        + diffusivity * laplacian
    )


def transport_kernel(
    diff_ref, keep_ref, select_ref, coarse_ref, below_ref, tile_ref, above_ref,
    out_ref,
    half_ref, wide_ref,
):
    block = tile_ref.shape[0]
    rows = tile_ref.shape[1]
    halo = below_ref.shape[1]
    frame = wide_ref.shape[0]
    pad = (frame - rows) // 2

    @pl.when(pl.program_id(0) == 0)
    def _():
        wide_ref[...] = jnp.zeros_like(wide_ref)
        for comp in range(half_ref.shape[0]):
            total = None
            for part in range(select_ref.shape[0]):
                term = jnp.concatenate(
                    [
                        jnp.dot(
                            select_ref[part, comp],
                            coarse_ref[:, step_index].reshape(-1, coarse_ref.shape[3]),
                            preferred_element_type=jnp.float32,
                        )
                        for step_index in range(coarse_ref.shape[1])
                    ],
                    axis=1,
                )
                total = term if total is None else total + term
            half_ref[comp] = total

    cells = tile_ref.shape[2]

    def half(step_index, comp):
        return half_ref[comp, :, pl.ds(step_index * cells, cells)]

    edge = lax.broadcasted_iota(jnp.int32, (pad, cells), 0)
    keep_top = (edge != pad - 1) | (keep_ref[0] != 0)
    keep_bottom = (edge != 0) | (keep_ref[1] != 0)

    def one_scalar(k, carry):
        index = pl.program_id(0) * block + k
        d = diff_ref[index]
        wide_ref[pl.ds(pad, rows), :] = tile_ref[k]
        wide_ref[pl.ds(pad - halo, halo), :] = below_ref[index]
        wide_ref[pl.ds(pad + rows, halo), :] = above_ref[index]
        first = advance(wide_ref[...], half(0, 0), half(0, 1), d, 0, frame)
        first = jnp.concatenate(
            [
                jnp.where(keep_top, first[:pad], 0.0),
                first[pad:pad + rows],
                jnp.where(keep_bottom, first[pad + rows:], 0.0),
            ],
            axis=0,
        )
        out_ref[k] = advance(first, half(1, 0), half(1, 1), d, pad, rows)
        return carry

    lax.fori_loop(0, block, one_scalar, 0)


def body(scalars, schmidt, velocity_history, fine_src, remap_weight, snap_step):
    scal_dev, tile_rows, cells = scalars.shape
    slot_count, comps, coarse_dev, _ = velocity_history.shape
    size = lambda name: lax.axis_size(name)
    tile_count = size("zl") * size("x")
    me = lax.axis_index("zl") * size("x") + lax.axis_index("x")
    anchor = me * tile_rows
    diffusivity = diffusion_scale / schmidt

    width = STEPS
    head = scalars[:, :width]
    tail = scalars[:, tile_rows - width:]

    owners = snap_step // slot_count
    slots = snap_step % slot_count
    owner_c = owners % size("c")
    owner_zh = (owners // size("c")) % size("zh")
    owner_y = owners // (size("c") * size("zh"))
    height = comps * coarse_dev

    def spread(block, count):
        return jnp.broadcast_to(block[None], (count,) + block.shape).reshape(-1, block.shape[1])

    core = lax.axis_index("c")
    by_row = velocity_history.reshape(slot_count * height, cells)
    per_core = jnp.stack(
        [lax.dynamic_slice_in_dim(by_row, slots[t] * height, height) for t in range(STEPS)]
    )

    spread_1 = jnp.broadcast_to(per_core[None], (size("y"),) + per_core.shape).reshape(-1, cells)
    first = lax.all_to_all(spread_1, ("y", "c"), 0, 0, tiled=True)
    first, head, tail, fine_src, remap_weight = lax.optimization_barrier(
        (first, head, tail, fine_src, remap_weight)
    )
    below = lax.ppermute(tail, SPACE, [(i, i + 1) for i in range(tile_count - 1)])
    above = lax.ppermute(head, SPACE, [(i + 1, i) for i in range(tile_count - 1)])
    core_y = lax.dynamic_index_in_dim(owner_y, core, keepdims=False)
    core_c = lax.dynamic_index_in_dim(owner_c, core, keepdims=False)
    mine = lax.dynamic_slice_in_dim(first, (core_y * size("c") + core_c) * height, height)
    core_zh = lax.dynamic_index_in_dim(owner_zh, core, keepdims=False)

    ring = size("zh") * size("zl")
    second = lax.all_to_all(spread(mine, ring), ("zh", "zl"), 0, 0, tiled=True)
    half_rows = size("zl") * height
    column = lax.dynamic_slice_in_dim(second, core_zh * half_rows, half_rows)

    coarse = lax.all_to_all(spread(column, size("x") * size("c")), ("x", "c"), 0, 0, tiled=True)
    coarse = coarse.reshape(size("x"), size("c"), half_rows, cells)
    coarse_rows = tile_count * coarse_dev

    frame = tile_rows + 16
    pad = (frame - tile_rows) // 2
    global_row = jnp.arange(frame, dtype=jnp.int32) + anchor - pad
    valid = (global_row >= 0) & (global_row < tile_rows * tile_count)
    clipped = jnp.clip(global_row, 0, tile_rows * tile_count - 1)
    src = jnp.where(valid, fine_src[clipped], -2)
    w = jnp.where(valid, remap_weight[clipped], 0.0)
    column_index = lax.broadcasted_iota(jnp.int32, (frame, coarse_rows), 1)
    select = jnp.where(column_index == src[:, None], (0.5 * (1.0 - w))[:, None], 0.0) + jnp.where(
        column_index == src[:, None] + 1, (0.5 * w)[:, None], 0.0
    )
    by_tile = select.reshape(frame, size("zl"), size("x"), coarse_dev).transpose(0, 2, 1, 3)
    select = jnp.stack(
        [
            jnp.stack(
                [by_tile if c == comp else jnp.zeros_like(by_tile) for c in range(comps)], axis=3
            ).reshape(frame, coarse_rows * comps)
            for comp in range(comps)
        ]
    )
    parts = []
    rest = select
    for _ in range(3):
        piece = lax.reduce_precision(rest, exponent_bits=8, mantissa_bits=7)
        parts.append(piece.astype(jnp.bfloat16))
        rest = rest - piece
    select = jnp.stack(parts)
    keep = jnp.stack([me > 0, me < tile_count - 1]).astype(jnp.int32)

    block = 16 if scal_dev % 16 == 0 else 1
    smem = pl.BlockSpec(memory_space=pltpu.SMEM)
    vmem = pl.BlockSpec(memory_space=pltpu.VMEM)
    tile_spec = pl.BlockSpec((block, tile_rows, cells), lambda i: (i, 0, 0))
    return pl.pallas_call(
        transport_kernel,
        grid=(scal_dev // block,),
        in_specs=[
            smem, smem,
            pl.BlockSpec(select.shape, lambda i: (0,) * select.ndim),
            vmem,
            vmem, tile_spec, vmem,
        ],
        out_specs=tile_spec,
        out_shape=jax.ShapeDtypeStruct(scalars.shape, scalars.dtype),
        scratch_shapes=[
            pltpu.VMEM((comps, frame, STEPS * cells), jnp.float32),
            pltpu.VMEM((frame, cells), jnp.float32),
        ],
        compiler_params=pltpu.CompilerParams(dimension_semantics=("arbitrary",)),
    )(diffusivity, keep, select, coarse, below, scalars, above)


SPACE = ("zl", "x")
SCAL = ("y", "zh", "c")


def solution(mesh):
    space, scal = mesh.shape["space"], mesh.shape["scal"]
    devices = mesh.devices.reshape(space // 4, 4, scal // 4, 2, 2)
    named = jax.sharding.Mesh(devices, SPACE + SCAL)
    return jax.shard_map(
        body,
        mesh=named,
        in_specs=(
            P(SCAL, SPACE, None),
            P(SCAL),
            P(SCAL, None, SPACE, None),
            P(),
            P(),
            P(),
        ),
        out_specs=P(SCAL, SPACE, None),
        check_vma=False,
    )
```

```python
import jax
import jax.numpy as jnp
from jax import lax
from jax.experimental import pallas as pl
from jax.experimental.pallas import tpu as pltpu
from jax.sharding import PartitionSpec as P

STEPS = 2


diffusion_scale = 0.24


def advance(center, half_0, half_1, diffusivity, start, count):
    rows, cells = center.shape
    upper_row = pltpu.roll(center, rows - 1, 0)[start:start + count]
    lower_row = pltpu.roll(center, 1, 0)[start:start + count]
    east_cell = pltpu.roll(center, cells - 1, 1)[start:start + count]
    west_cell = pltpu.roll(center, 1, 1)[start:start + count]
    center = center[start:start + count]
    neighbours = upper_row + lower_row + east_cell + west_cell
    return (
        center * (1.0 - 4.0 * diffusivity)
        + diffusivity * neighbours
        - half_0[start:start + count] * (upper_row - lower_row)
        - half_1[start:start + count] * (east_cell - west_cell)
    )


def transport_kernel(
    diff_ref, keep_ref, select_ref, coarse_ref, below_ref, tile_ref, above_ref,
    out_ref,
    half_ref, wide_ref,
):
    block = tile_ref.shape[0]
    rows = tile_ref.shape[1]
    halo = below_ref.shape[1]
    frame = wide_ref.shape[0]
    pad = (frame - rows) // 2

    @pl.when(pl.program_id(0) == 0)
    def _():
        wide_ref[...] = jnp.zeros_like(wide_ref)
        for comp in range(half_ref.shape[0]):
            total = None
            for part in range(select_ref.shape[0]):
                term = jnp.concatenate(
                    [
                        jnp.dot(
                            select_ref[part, comp],
                            coarse_ref[:, step_index].reshape(-1, coarse_ref.shape[3]),
                            preferred_element_type=jnp.float32,
                        )
                        for step_index in range(coarse_ref.shape[1])
                    ],
                    axis=1,
                )
                total = term if total is None else total + term
            half_ref[comp] = total

    cells = tile_ref.shape[2]

    def half(step_index, comp):
        return half_ref[comp, :, pl.ds(step_index * cells, cells)]

    edge = lax.broadcasted_iota(jnp.int32, (pad, cells), 0)
    keep_top = (edge != pad - 1) | (keep_ref[0] != 0)
    keep_bottom = (edge != 0) | (keep_ref[1] != 0)

    def one_scalar(k, carry):
        index = pl.program_id(0) * block + k
        d = diff_ref[index]
        wide_ref[pl.ds(pad, rows), :] = tile_ref[k]
        wide_ref[pl.ds(pad - halo, halo), :] = below_ref[index]
        wide_ref[pl.ds(pad + rows, halo), :] = above_ref[index]
        first = advance(wide_ref[...], half(0, 0), half(0, 1), d, 0, frame)
        first = jnp.concatenate(
            [
                jnp.where(keep_top, first[:pad], 0.0),
                first[pad:pad + rows],
                jnp.where(keep_bottom, first[pad + rows:], 0.0),
            ],
            axis=0,
        )
        out_ref[k] = advance(first, half(1, 0), half(1, 1), d, pad, rows)
        return carry

    lax.fori_loop(0, block, one_scalar, 0)


def body(scalars, schmidt, velocity_history, fine_src, remap_weight, snap_step):
    scal_dev, tile_rows, cells = scalars.shape
    slot_count, comps, coarse_dev, _ = velocity_history.shape
    size = lambda name: lax.axis_size(name)
    tile_count = size("zl") * size("x")
    me = lax.axis_index("zl") * size("x") + lax.axis_index("x")
    anchor = me * tile_rows
    diffusivity = diffusion_scale / schmidt

    width = STEPS
    head = scalars[:, :width]
    tail = scalars[:, tile_rows - width:]

    owners = snap_step // slot_count
    slots = snap_step % slot_count
    owner_c = owners % size("c")
    owner_zh = (owners // size("c")) % size("zh")
    owner_y = owners // (size("c") * size("zh"))
    height = comps * coarse_dev

    def spread(block, count):
        return jnp.broadcast_to(block[None], (count,) + block.shape).reshape(-1, block.shape[1])

    by_row = velocity_history.reshape(slot_count * height, cells)
    peers = size("y") * size("c")
    first = lax.all_to_all(spread(by_row, peers), ("y", "c"), 0, 0, tiled=True)
    first, head, tail, fine_src, remap_weight = lax.optimization_barrier(
        (first, head, tail, fine_src, remap_weight)
    )
    below = lax.ppermute(tail, SPACE, [(i, i + 1) for i in range(tile_count - 1)])
    above = lax.ppermute(head, SPACE, [(i + 1, i) for i in range(tile_count - 1)])
    local = jnp.concatenate(
        [
            lax.dynamic_slice_in_dim(
                first,
                ((owner_y[t] * size("c") + owner_c[t]) * slot_count + slots[t]) * height,
                height,
            )
            for t in range(STEPS)
        ],
        axis=1,
    )

    core = lax.axis_index("c")
    mine = lax.dynamic_slice_in_dim(local, core * cells, cells, axis=1)
    core_zh = lax.dynamic_index_in_dim(owner_zh, core, keepdims=False)

    ring = size("zh") * size("zl")
    second = lax.all_to_all(spread(mine, ring), ("zh", "zl"), 0, 0, tiled=True)
    half_rows = size("zl") * height
    column = lax.dynamic_slice_in_dim(second, core_zh * half_rows, half_rows)

    coarse = lax.all_to_all(spread(column, size("x") * size("c")), ("x", "c"), 0, 0, tiled=True)
    coarse = coarse.reshape(size("x"), size("c"), half_rows, cells)
    coarse_rows = tile_count * coarse_dev

    frame = tile_rows + 16
    pad = (frame - tile_rows) // 2
    global_row = jnp.arange(frame, dtype=jnp.int32) + anchor - pad
    valid = (global_row >= 0) & (global_row < tile_rows * tile_count)
    clipped = jnp.clip(global_row, 0, tile_rows * tile_count - 1)
    src = jnp.where(valid, fine_src[clipped], -2)
    w = jnp.where(valid, remap_weight[clipped], 0.0)
    column_index = lax.broadcasted_iota(jnp.int32, (frame, coarse_rows), 1)
    select = jnp.where(column_index == src[:, None], (0.5 * (1.0 - w))[:, None], 0.0) + jnp.where(
        column_index == src[:, None] + 1, (0.5 * w)[:, None], 0.0
    )
    by_tile = select.reshape(frame, size("zl"), size("x"), coarse_dev).transpose(0, 2, 1, 3)
    select = jnp.stack(
        [
            jnp.stack(
                [by_tile if c == comp else jnp.zeros_like(by_tile) for c in range(comps)], axis=3
            ).reshape(frame, coarse_rows * comps)
            for comp in range(comps)
        ]
    )
    parts = []
    rest = select
    for _ in range(3):
        piece = lax.reduce_precision(rest, exponent_bits=8, mantissa_bits=7)
        parts.append(piece.astype(jnp.bfloat16))
        rest = rest - piece
    select = jnp.stack(parts)
    keep = jnp.stack([me > 0, me < tile_count - 1]).astype(jnp.int32)

    block = 16 if scal_dev % 16 == 0 else 1
    smem = pl.BlockSpec(memory_space=pltpu.SMEM)
    vmem = pl.BlockSpec(memory_space=pltpu.VMEM)
    tile_spec = pl.BlockSpec((block, tile_rows, cells), lambda i: (i, 0, 0))
    return pl.pallas_call(
        transport_kernel,
        grid=(scal_dev // block,),
        in_specs=[
            smem, smem,
            pl.BlockSpec(select.shape, lambda i: (0,) * select.ndim),
            vmem,
            vmem, tile_spec, vmem,
        ],
        out_specs=tile_spec,
        out_shape=jax.ShapeDtypeStruct(scalars.shape, scalars.dtype),
        scratch_shapes=[
            pltpu.VMEM((comps, frame, STEPS * cells), jnp.float32),
            pltpu.VMEM((frame, cells), jnp.float32),
        ],
        compiler_params=pltpu.CompilerParams(dimension_semantics=("arbitrary",)),
    )(diffusivity, keep, select, coarse, below, scalars, above)


SPACE = ("zl", "x")
SCAL = ("y", "zh", "c")


def solution(mesh):
    space, scal = mesh.shape["space"], mesh.shape["scal"]
    devices = mesh.devices.reshape(space // 4, 4, scal // 4, 2, 2)
    named = jax.sharding.Mesh(devices, SPACE + SCAL)
    return jax.shard_map(
        body,
        mesh=named,
        in_specs=(
            P(SCAL, SPACE, None),
            P(SCAL),
            P(SCAL, None, SPACE, None),
            P(),
            P(),
            P(),
        ),
        out_specs=P(SCAL, SPACE, None),
        check_vma=False,
    )
```

```python
import jax
import jax.numpy as jnp
from jax import lax
from jax.experimental import pallas as pl
from jax.experimental.pallas import tpu as pltpu
from jax.sharding import PartitionSpec as P

STEPS = 2


diffusion_scale = 0.24


def advance(center, half_0, half_1, diffusivity, start, count):
    rows, cells = center.shape
    upper_row = pltpu.roll(center, rows - 1, 0)[start:start + count]
    lower_row = pltpu.roll(center, 1, 0)[start:start + count]
    east_cell = pltpu.roll(center, cells - 1, 1)[start:start + count]
    west_cell = pltpu.roll(center, 1, 1)[start:start + count]
    center = center[start:start + count]
    laplacian = upper_row + lower_row + east_cell + west_cell - 4.0 * center
    return (
        center
        - half_0[start:start + count] * (upper_row - lower_row)
        - half_1[start:start + count] * (east_cell - west_cell)
        + diffusivity * laplacian
    )


def transport_kernel(
    diff_ref, keep_ref, select_ref, coarse_ref, below_ref, tile_ref, above_ref,
    out_ref,
    half_ref, wide_ref,
):
    block = tile_ref.shape[0]
    rows = tile_ref.shape[1]
    halo = below_ref.shape[1]
    frame = wide_ref.shape[0]
    pad = (frame - rows) // 2

    @pl.when(pl.program_id(0) == 0)
    def _():
        wide_ref[...] = jnp.zeros_like(wide_ref)
        for comp in range(half_ref.shape[0]):
            total = None
            for part in range(select_ref.shape[0]):
                term = jnp.concatenate(
                    [
                        jnp.dot(
                            select_ref[part, comp],
                            coarse_ref[:, step_index].reshape(-1, coarse_ref.shape[3]),
                            preferred_element_type=jnp.float32,
                        )
                        for step_index in range(coarse_ref.shape[1])
                    ],
                    axis=1,
                )
                total = term if total is None else total + term
            half_ref[comp] = total

    cells = tile_ref.shape[2]

    def half(step_index, comp):
        return half_ref[comp, :, pl.ds(step_index * cells, cells)]

    edge = lax.broadcasted_iota(jnp.int32, (pad, cells), 0)
    keep_top = (edge != pad - 1) | (keep_ref[0] != 0)
    keep_bottom = (edge != 0) | (keep_ref[1] != 0)

    def one_scalar(k, carry):
        index = pl.program_id(0) * block + k
        d = diff_ref[index]
        wide_ref[pl.ds(pad, rows), :] = tile_ref[k]
        wide_ref[pl.ds(pad - halo, halo), :] = below_ref[index]
        wide_ref[pl.ds(pad + rows, halo), :] = above_ref[index]
        first = advance(wide_ref[...], half(0, 0), half(0, 1), d, 0, frame)
        first = jnp.concatenate(
            [
                jnp.where(keep_top, first[:pad], 0.0),
                first[pad:pad + rows],
                jnp.where(keep_bottom, first[pad + rows:], 0.0),
            ],
            axis=0,
        )
        out_ref[k] = advance(first, half(1, 0), half(1, 1), d, pad, rows)
        return carry

    lax.fori_loop(0, block, one_scalar, 0)


def body(scalars, schmidt, velocity_history, fine_src, remap_weight, snap_step):
    scal_dev, tile_rows, cells = scalars.shape
    slot_count, comps, coarse_dev, _ = velocity_history.shape
    size = lambda name: lax.axis_size(name)
    tile_count = size("zl") * size("x")
    me = lax.axis_index("zl") * size("x") + lax.axis_index("x")
    anchor = me * tile_rows
    diffusivity = diffusion_scale / schmidt

    width = STEPS
    head = scalars[:, :width]
    tail = scalars[:, tile_rows - width:]

    owners = snap_step // slot_count
    slots = snap_step % slot_count
    owner_c = owners % size("c")
    owner_zh = (owners // size("c")) % size("zh")
    owner_y = owners // (size("c") * size("zh"))
    height = comps * coarse_dev

    def spread(block, count):
        return jnp.broadcast_to(block[None], (count,) + block.shape).reshape(-1, block.shape[1])

    by_row = velocity_history.reshape(slot_count * height, cells)
    peers = size("y") * size("c")
    first = lax.all_to_all(spread(by_row, peers), ("y", "c"), 0, 0, tiled=True)
    first, head, tail, fine_src, remap_weight = lax.optimization_barrier(
        (first, head, tail, fine_src, remap_weight)
    )
    below = lax.ppermute(tail, SPACE, [(i, i + 1) for i in range(tile_count - 1)])
    above = lax.ppermute(head, SPACE, [(i + 1, i) for i in range(tile_count - 1)])
    local = jnp.concatenate(
        [
            lax.dynamic_slice_in_dim(
                first,
                ((owner_y[t] * size("c") + owner_c[t]) * slot_count + slots[t]) * height,
                height,
            )
            for t in range(STEPS)
        ],
        axis=1,
    )

    core = lax.axis_index("c")
    mine = lax.dynamic_slice_in_dim(local, core * cells, cells, axis=1)
    core_zh = lax.dynamic_index_in_dim(owner_zh, core, keepdims=False)

    ring = size("zh") * size("zl")
    second = lax.all_to_all(spread(mine, ring), ("zh", "zl"), 0, 0, tiled=True)
    half_rows = size("zl") * height
    column = lax.dynamic_slice_in_dim(second, core_zh * half_rows, half_rows)

    coarse = lax.all_to_all(spread(column, size("x") * size("c")), ("x", "c"), 0, 0, tiled=True)
    coarse = coarse.reshape(size("x"), size("c"), half_rows, cells)
    coarse_rows = tile_count * coarse_dev

    frame = tile_rows + 16
    pad = (frame - tile_rows) // 2
    global_row = jnp.arange(frame, dtype=jnp.int32) + anchor - pad
    valid = (global_row >= 0) & (global_row < tile_rows * tile_count)
    clipped = jnp.clip(global_row, 0, tile_rows * tile_count - 1)
    src = jnp.where(valid, fine_src[clipped], -2)
    w = jnp.where(valid, remap_weight[clipped], 0.0)
    column_index = lax.broadcasted_iota(jnp.int32, (frame, coarse_rows), 1)
    select = jnp.where(column_index == src[:, None], (0.5 * (1.0 - w))[:, None], 0.0) + jnp.where(
        column_index == src[:, None] + 1, (0.5 * w)[:, None], 0.0
    )
    by_tile = select.reshape(frame, size("zl"), size("x"), coarse_dev).transpose(0, 2, 1, 3)
    select = jnp.stack(
        [
            jnp.stack(
                [by_tile if c == comp else jnp.zeros_like(by_tile) for c in range(comps)], axis=3
            ).reshape(frame, coarse_rows * comps)
            for comp in range(comps)
        ]
    )
    parts = []
    rest = select
    for _ in range(3):
        piece = lax.reduce_precision(rest, exponent_bits=8, mantissa_bits=7)
        parts.append(piece.astype(jnp.bfloat16))
        rest = rest - piece
    select = jnp.stack(parts)
    keep = jnp.stack([me > 0, me < tile_count - 1]).astype(jnp.int32)

    block = 8 if scal_dev % 8 == 0 else 1
    smem = pl.BlockSpec(memory_space=pltpu.SMEM)
    vmem = pl.BlockSpec(memory_space=pltpu.VMEM)
    tile_spec = pl.BlockSpec((block, tile_rows, cells), lambda i: (i, 0, 0))
    return pl.pallas_call(
        transport_kernel,
        grid=(scal_dev // block,),
        in_specs=[
            smem, smem,
            pl.BlockSpec(select.shape, lambda i: (0,) * select.ndim),
            vmem,
            vmem, tile_spec, vmem,
        ],
        out_specs=tile_spec,
        out_shape=jax.ShapeDtypeStruct(scalars.shape, scalars.dtype),
        scratch_shapes=[
            pltpu.VMEM((comps, frame, STEPS * cells), jnp.float32),
            pltpu.VMEM((frame, cells), jnp.float32),
        ],
        compiler_params=pltpu.CompilerParams(dimension_semantics=("arbitrary",)),
    )(diffusivity, keep, select, coarse, below, scalars, above)


SPACE = ("zl", "x")
SCAL = ("y", "zh", "c")


def solution(mesh):
    space, scal = mesh.shape["space"], mesh.shape["scal"]
    devices = mesh.devices.reshape(space // 4, 4, scal // 4, 2, 2)
    named = jax.sharding.Mesh(devices, SPACE + SCAL)
    return jax.shard_map(
        body,
        mesh=named,
        in_specs=(
            P(SCAL, SPACE, None),
            P(SCAL),
            P(SCAL, None, SPACE, None),
            P(),
            P(),
            P(),
        ),
        out_specs=P(SCAL, SPACE, None),
        check_vma=False,
    )
```

```python
import jax
import jax.numpy as jnp
from jax import lax
from jax.experimental import pallas as pl
from jax.experimental.pallas import tpu as pltpu
from jax.sharding import PartitionSpec as P

STEPS = 2


diffusion_scale = 0.24


def advance(center, half_0, half_1, diffusivity, start, count):
    rows, cells = center.shape
    upper_row = pltpu.roll(center, rows - 1, 0)[start:start + count]
    lower_row = pltpu.roll(center, 1, 0)[start:start + count]
    east_cell = pltpu.roll(center, cells - 1, 1)[start:start + count]
    west_cell = pltpu.roll(center, 1, 1)[start:start + count]
    center = center[start:start + count]
    laplacian = upper_row + lower_row + east_cell + west_cell - 4.0 * center
    return (
        center
        - half_0[start:start + count] * (upper_row - lower_row)
        - half_1[start:start + count] * (east_cell - west_cell)
        + diffusivity * laplacian
    )


def transport_kernel(
    diff_ref, keep_ref, select_ref, coarse_ref, below_ref, tile_ref, above_ref,
    out_ref,
    half_ref, wide_ref,
):
    block = tile_ref.shape[0]
    rows = tile_ref.shape[1]
    halo = below_ref.shape[1]
    frame = wide_ref.shape[0]
    pad = (frame - rows) // 2

    @pl.when(pl.program_id(0) == 0)
    def _():
        wide_ref[...] = jnp.zeros_like(wide_ref)
        for comp in range(half_ref.shape[0]):
            total = None
            for part in range(select_ref.shape[0]):
                term = jnp.concatenate(
                    [
                        jnp.dot(
                            select_ref[part, comp],
                            coarse_ref[:, step_index].reshape(-1, coarse_ref.shape[3]),
                            preferred_element_type=jnp.float32,
                        )
                        for step_index in range(coarse_ref.shape[1])
                    ],
                    axis=1,
                )
                total = term if total is None else total + term
            half_ref[comp] = total

    cells = tile_ref.shape[2]

    def half(step_index, comp):
        return half_ref[comp, :, pl.ds(step_index * cells, cells)]

    edge = lax.broadcasted_iota(jnp.int32, (pad, cells), 0)
    keep_top = (edge != pad - 1) | (keep_ref[0] != 0)
    keep_bottom = (edge != 0) | (keep_ref[1] != 0)

    def one_scalar(k, carry):
        index = pl.program_id(0) * block + k
        d = diff_ref[index]
        wide_ref[pl.ds(pad, rows), :] = tile_ref[k]
        wide_ref[pl.ds(pad - halo, halo), :] = below_ref[index]
        wide_ref[pl.ds(pad + rows, halo), :] = above_ref[index]
        first = advance(wide_ref[...], half(0, 0), half(0, 1), d, 0, frame)
        first = jnp.concatenate(
            [
                jnp.where(keep_top, first[:pad], 0.0),
                first[pad:pad + rows],
                jnp.where(keep_bottom, first[pad + rows:], 0.0),
            ],
            axis=0,
        )
        out_ref[k] = advance(first, half(1, 0), half(1, 1), d, pad, rows)
        return carry

    lax.fori_loop(0, block, one_scalar, 0)


def body(scalars, schmidt, velocity_history, fine_src, remap_weight, snap_step):
    scal_dev, tile_rows, cells = scalars.shape
    slot_count, comps, coarse_dev, _ = velocity_history.shape
    size = lambda name: lax.axis_size(name)
    tile_count = size("zl") * size("x")
    me = lax.axis_index("zl") * size("x") + lax.axis_index("x")
    anchor = me * tile_rows
    diffusivity = diffusion_scale / schmidt

    width = STEPS
    head = scalars[:, :width]
    tail = scalars[:, tile_rows - width:]

    owners = snap_step // slot_count
    slots = snap_step % slot_count
    owner_c = owners % size("c")
    owner_zh = (owners // size("c")) % size("zh")
    owner_y = owners // (size("c") * size("zh"))
    height = comps * coarse_dev

    def spread(block, count):
        return jnp.broadcast_to(block[None], (count,) + block.shape).reshape(-1, block.shape[1])

    by_row = velocity_history.reshape(slot_count * height, cells)
    peers = size("y") * size("c")
    first = lax.all_to_all(spread(by_row, peers), ("y", "c"), 0, 0, tiled=True)
    first, head, tail, fine_src, remap_weight = lax.optimization_barrier(
        (first, head, tail, fine_src, remap_weight)
    )
    below = lax.ppermute(tail, SPACE, [(i, i + 1) for i in range(tile_count - 1)])
    above = lax.ppermute(head, SPACE, [(i + 1, i) for i in range(tile_count - 1)])
    local = jnp.concatenate(
        [
            lax.dynamic_slice_in_dim(
                first,
                ((owner_y[t] * size("c") + owner_c[t]) * slot_count + slots[t]) * height,
                height,
            )
            for t in range(STEPS)
        ],
        axis=1,
    )

    core = lax.axis_index("c")
    mine = lax.dynamic_slice_in_dim(local, core * cells, cells, axis=1)
    core_zh = lax.dynamic_index_in_dim(owner_zh, core, keepdims=False)

    ring = size("zh") * size("zl")
    second = lax.all_to_all(spread(mine, ring), ("zh", "zl"), 0, 0, tiled=True)
    half_rows = size("zl") * height
    column = lax.dynamic_slice_in_dim(second, core_zh * half_rows, half_rows)

    coarse = lax.all_to_all(spread(column, size("x") * size("c")), ("x", "c"), 0, 0, tiled=True)
    coarse = coarse.reshape(size("x"), size("c"), half_rows, cells)
    coarse_rows = tile_count * coarse_dev

    frame = tile_rows + 16
    pad = (frame - tile_rows) // 2
    global_row = jnp.arange(frame, dtype=jnp.int32) + anchor - pad
    valid = (global_row >= 0) & (global_row < tile_rows * tile_count)
    clipped = jnp.clip(global_row, 0, tile_rows * tile_count - 1)
    src = jnp.where(valid, fine_src[clipped], -2)
    w = jnp.where(valid, remap_weight[clipped], 0.0)
    column_index = lax.broadcasted_iota(jnp.int32, (frame, coarse_rows), 1)
    select = jnp.where(column_index == src[:, None], (0.5 * (1.0 - w))[:, None], 0.0) + jnp.where(
        column_index == src[:, None] + 1, (0.5 * w)[:, None], 0.0
    )
    by_tile = select.reshape(frame, size("zl"), size("x"), coarse_dev).transpose(0, 2, 1, 3)
    select = jnp.stack(
        [
            jnp.stack(
                [by_tile if c == comp else jnp.zeros_like(by_tile) for c in range(comps)], axis=3
            ).reshape(frame, coarse_rows * comps)
            for comp in range(comps)
        ]
    )
    parts = []
    rest = select
    for _ in range(3):
        piece = lax.reduce_precision(rest, exponent_bits=8, mantissa_bits=7)
        parts.append(piece.astype(jnp.bfloat16))
        rest = rest - piece
    select = jnp.stack(parts)
    keep = jnp.stack([me > 0, me < tile_count - 1]).astype(jnp.int32)

    block = 4 if scal_dev % 4 == 0 else 1
    smem = pl.BlockSpec(memory_space=pltpu.SMEM)
    vmem = pl.BlockSpec(memory_space=pltpu.VMEM)
    tile_spec = pl.BlockSpec((block, tile_rows, cells), lambda i: (i, 0, 0))
    return pl.pallas_call(
        transport_kernel,
        grid=(scal_dev // block,),
        in_specs=[
            smem, smem,
            pl.BlockSpec(select.shape, lambda i: (0,) * select.ndim),
            vmem,
            vmem, tile_spec, vmem,
        ],
        out_specs=tile_spec,
        out_shape=jax.ShapeDtypeStruct(scalars.shape, scalars.dtype),
        scratch_shapes=[
            pltpu.VMEM((comps, frame, STEPS * cells), jnp.float32),
            pltpu.VMEM((frame, cells), jnp.float32),
        ],
        compiler_params=pltpu.CompilerParams(dimension_semantics=("arbitrary",)),
    )(diffusivity, keep, select, coarse, below, scalars, above)


SPACE = ("zl", "x")
SCAL = ("y", "zh", "c")


def solution(mesh):
    space, scal = mesh.shape["space"], mesh.shape["scal"]
    devices = mesh.devices.reshape(space // 4, 4, scal // 4, 2, 2)
    named = jax.sharding.Mesh(devices, SPACE + SCAL)
    return jax.shard_map(
        body,
        mesh=named,
        in_specs=(
            P(SCAL, SPACE, None),
            P(SCAL),
            P(SCAL, None, SPACE, None),
            P(),
            P(),
            P(),
        ),
        out_specs=P(SCAL, SPACE, None),
        check_vma=False,
    )
```
